32 devices in a mesh: dp: 4 (over y, x), expert: 8 (over z, core).
Axes of the slice: x: 2, y: 2, z: 4, core: 2. Of those that a mesh axis runs over, the one named last changes fastest.
Arguments:
- tokens: bfloat16 [4096, 2048], P(('dp', 'expert')), may hold values from -6 to 6
- cotangent: bfloat16 [4096, 2048], P(('dp', 'expert')), may hold values from -6 to 6
- expert_ids: int32 [4096, 4], P(('dp', 'expert')), may hold values from 0 to 7, all different within a row; in each aligned block of 128 rows (0 to 127, 128 to 255, ...) at most 96 rows name the same one
- gate_probs: float32 [4096, 4], P(('dp', 'expert')), may hold values from 0.05 to 1
- up_weight: bfloat16 [8, 2048, 768], P('expert', None, 'dp'), may hold values from -0.125 to 0.125
- down_weight: float32 [8, 768, 2048], P('expert', 'dp'), may hold values from -28 to 28
- moment1: float32 [8, 768, 2048], P('expert', 'dp'), may hold values from -60 to 60
- moment2: float32 [8, 768, 2048], P('expert', 'dp'), may hold values from 0.05 to 5
- pair_match: int32 [8], replicated, may hold values from 0 to 7, as said below
Outputs:
- down_out: float32 [8, 768, 2048], P('expert', 'dp')
- moment1_out: float32 [8, 768, 2048], P('expert', 'dp')
- moment2_out: float32 [8, 768, 2048], P('expert', 'dp')
The draws below stay inside these ranges and needn't reach their ends.
Inputs may be any that keep to these rules, and one draw needn't show every extreme that they name: `expert_ids`: each row names 4 different experts. Within the rows of one device (aligned blocks of 128 rows) no expert is named by more than 96 rows, a bound that some block reaches. A perfect matching: pair_match[pair_match[i]] = i and pair_match[i] != i for every i.
All inputs are finite; a program needn't handle non-finite values.
Results may differ from the reference program's by a relative error of at most 0.00035.
Values may be sent and summed in bfloat16 or wider, within the bound.
No kernel may reach another device: no remote copies, remote signals or barrier semaphores. Data moves between devices by JAX's collectives and lax.ppermute only.
A program may use at most 128 MiB of HBM per device.

```python
import math
import jax
import jax.numpy as jnp
import numpy as np
from jax import lax

D = 2048
FFN = 768
TOK_DEV = 128
EXPERTS = 8
TOP = 4
CAP = 96
TOKENS = 4096
N_DP = 4


def draw_pair_match(key, part):
    ordering = jax.random.permutation(key, EXPERTS).astype(jnp.int32)
    flipped = ordering.reshape(EXPERTS // 2, 2)[:, ::-1].reshape(EXPERTS)
    return jnp.zeros((EXPERTS,), jnp.int32).at[ordering].set(flipped)


def draw_down_weight(key, part):
    key_noise = jax.random.fold_in(key, 11)
    key_rows = jax.random.fold_in(key, 12)
    key_cols = jax.random.fold_in(key, 13)
    position = jnp.arange(FFN, dtype=jnp.float32) / FFN
    top_scale = 4.0
    noise = jnp.clip(jax.random.normal(key_noise, (EXPERTS, FFN, D), jnp.float32), -4.0, 4.0)
    row_scale = jnp.exp(jnp.log(top_scale) * position)
    row_factor = jax.random.uniform(key_rows, (EXPERTS, FFN, 1), jnp.float32, 0.7, 1.4)
    col_factor = jnp.exp(jax.random.uniform(key_cols, (EXPERTS, 1, D), jnp.float32, -0.6931, 0.6931))
    return 0.25 * noise * row_scale[None, :, None] * row_factor * col_factor


def shard_levels(rng, extent, pieces, smallest, high):
    gain = 1.0
    for dim, parts in pieces:
        steps = jax.random.uniform(jax.random.fold_in(jax.random.fold_in(rng, 6), dim), (parts,), jnp.float32, smallest / len(pieces), high / len(pieces))
        gain = gain * jnp.repeat(jnp.exp(steps), extent[dim] // parts).reshape((-1,) + (1,) * (len(extent) - 1 - dim))
    return gain


def deal_out(own_key, own, number, rows, amount, top, bound, lean):
    sequence = jax.random.permutation(own_key, amount)
    crowded, common = portions_of(amount, rows * top, bound, lean, True), portions_of(amount, rows * top, bound, lean, False)
    places = jnp.arange(amount)

    def named(sizes, rotation):
        used = int((sizes > 0).sum())
        fixed = max(1, used // 4)
        moved = fixed + (places - fixed + rotation * (used - fixed)) % max(1, amount - fixed)
        return jnp.zeros((amount,), jnp.int32).at[sequence[jnp.where(places < fixed, places, moved)]].set(jnp.asarray(sizes, jnp.int32))

    sizes = jnp.where(number % 4 == 0, named(crowded, number // 4), named(common, number - number // 4 - 1))
    mixed = jax.random.permutation(jax.random.fold_in(own, 3), amount)
    donor, taker = mixed[0:amount // 2 * 2:2], mixed[1:amount // 2 * 2:2]
    margin = jnp.minimum(sizes[donor] - 1, bound - sizes[taker]) // 2
    margin = jnp.where((donor == sequence[0]) | (taker == sequence[0]) | (sizes[taker] == 0), 0, jnp.maximum(margin, 0))
    moved = jax.random.randint(jax.random.fold_in(own, 4), (amount // 2,), 0, 1 << 20) % (margin + 1)
    sizes = sizes.at[donor].add(-moved).at[taker].add(moved)
    items = jnp.searchsorted(jnp.cumsum(sizes), jnp.arange(rows * top), side="right").astype(jnp.int32)
    listing = items.reshape(top, rows).T
    listing = listing[jax.random.permutation(jax.random.fold_in(own, 1), rows)]
    rotation = jax.random.randint(jax.random.fold_in(own, 2), (rows, 1), 0, top)
    return jnp.take_along_axis(listing, (jnp.arange(top)[None, :] + rotation) % top, axis=1)


def portions_of(number_of, total, reach, slope, full):
    portions = [(1 << 20) // math.isqrt(standing ** slope) + 1 for standing in range(1, number_of + 1)]
    largest = reach if full else min(reach, max(-(-total // number_of), total * portions[0] // sum(portions)))
    least = 1 if total - largest >= number_of - 1 else 0
    counts, rest = [largest] + [least] * (number_of - 1), total - largest - least * (number_of - 1)
    while rest > 0:
        candidates = [i for i in range(1, number_of) if counts[i] < largest] or [i for i in range(1, number_of) if counts[i] < reach]
        whole, left = sum([portions[i] for i in candidates]), rest
        for i in candidates:
            addition = min(reach - counts[i], max(1, left * portions[i] // whole), rest)
            counts[i] = counts[i] + addition
            rest = rest - addition
    return np.array(counts)


def bell_draw(stream_key, shape, scale, reach, pieces=(), held_as=jnp.bfloat16):
    result = scale * jax.random.normal(stream_key, shape, jnp.float32)
    if pieces:
        result = result * shard_levels(stream_key, shape, pieces, -0.22, 0.18)
    return jnp.clip(result, -reach, reach).astype(held_as)


def setup_inputs(seed: int = 0) -> dict:
    key_of = jax.random.split(jax.random.key(seed), 10)
    tokens = bell_draw(key_of[0], (TOKENS, D), 1.0, 6.0, ((0, 32),))
    cotangent = bell_draw(key_of[1], (TOKENS, D), 1.0, 6.0, ((0, 32),))
    expert_ids_keys = jax.random.split(jax.random.fold_in(key_of[2], 1), TOKENS // TOK_DEV)
    expert_ids_turns = jax.random.permutation(jax.random.fold_in(key_of[2], 3), TOKENS // TOK_DEV)
    expert_ids = jax.vmap(lambda own, number: deal_out(jax.random.fold_in(key_of[2], 2), own, number, TOK_DEV, EXPERTS, TOP, CAP, 2))(expert_ids_keys, expert_ids_turns).reshape((TOKENS, TOP))
    gate_probs = jnp.clip(jnp.exp(math.log(1.0) - 2.9957323 * jax.random.uniform(key_of[3], (TOKENS, TOP), jnp.float32) ** shard_levels(key_of[3], (TOKENS, TOP), ((0, 32),), -0.2, 0.2)), 0.05, 1.0)
    up_weight = bell_draw(key_of[4], (EXPERTS, D, FFN), D ** -0.5, 0.125, ((0, 8), (2, 4)))
    down_weight = draw_down_weight(jax.random.fold_in(key_of[9], 71), 0)
    moment1 = bell_draw(key_of[6], (EXPERTS, FFN, D), 10.0, 60.0, ((0, 8), (1, 4)), jnp.float32)
    moment2 = jnp.clip(jnp.exp(math.log(5.0) - 4.6051702 * jax.random.uniform(key_of[7], (EXPERTS, FFN, D), jnp.float32) ** shard_levels(key_of[7], (EXPERTS, FFN, D), ((0, 8), (1, 4)), -0.2, 0.2)), 0.05, 5.0)
    pair_match = draw_pair_match(jax.random.fold_in(key_of[9], 71), 0)
    return dict(tokens=tokens, cotangent=cotangent, expert_ids=expert_ids, gate_probs=gate_probs, up_weight=up_weight, down_weight=down_weight, moment1=moment1, moment2=moment2, pair_match=pair_match)


beta_one = 0.9
beta_two = 0.999
epsilon = 1e-06
learn_rate = 0.05

def reference(tokens, cotangent, expert_ids, gate_probs, up_weight, down_weight, moment1, moment2, pair_match):
    most_rows = N_DP * EXPERTS * CAP
    flat_ids = expert_ids.reshape(-1)
    flat_probs = gate_probs.reshape(-1)
    flat_rows = (jnp.arange(TOKENS * TOP, dtype=jnp.int32) // TOP).astype(jnp.int32)

    def one_expert(expert):
        matched = flat_ids == expert
        ordering = jnp.argsort(jnp.where(matched, 0, 1).astype(jnp.int32), stable=True)[:most_rows].astype(jnp.int32)
        chosen = matched[ordering]
        row_index = flat_rows[ordering]
        gathered = tokens[row_index]
        weights_row = jnp.where(chosen, flat_probs[ordering], jnp.float32(0.0))
        scaled = (weights_row[:, None] * cotangent[row_index].astype(jnp.float32)).astype(jnp.bfloat16)
        pre_act = jnp.dot(gathered, up_weight[expert], preferred_element_type=jnp.float32)
        hidden = jax.nn.silu(pre_act).astype(jnp.bfloat16)
        return jnp.dot(hidden.T, scaled, preferred_element_type=jnp.float32)
    gradient = lax.map(one_expert, jnp.arange(EXPERTS, dtype=jnp.int32))
    first = beta_one * moment1 + (1.0 - beta_one) * gradient
    second = beta_two * moment2 + (1.0 - beta_two) * gradient * gradient
    update = first / (jnp.sqrt(second) + epsilon)
    weight_norm = jnp.sqrt(lax.optimization_barrier(jnp.sum(down_weight * down_weight, axis=(1, 2))))
    update_norm = jnp.sqrt(lax.optimization_barrier(jnp.sum(update * update, axis=(1, 2))))
    trust = weight_norm / (update_norm + epsilon)
    renewed = down_weight - learn_rate * trust[:, None, None] * update
    return (renewed[pair_match], first[pair_match], second[pair_match])
```

```python
import jax
import jax.numpy as jnp
from jax import lax
from jax.sharding import PartitionSpec as P

beta_one = 0.9
beta_two = 0.999
epsilon = 1e-06
learn_rate = 0.05

dense_rows_max = 2048


def relocate(states, pair_match):
    group_size = lax.axis_size("expert")
    count_states = len(states)
    stacked = jnp.stack(states).reshape(count_states, group_size, -1)
    chosen = jnp.take(
        lax.all_to_all(stacked, "expert", split_axis=1, concat_axis=1, tiled=True),
        pair_match,
        axis=1,
    )
    arrived = lax.all_to_all(chosen, "expert", split_axis=1, concat_axis=1, tiled=True)
    arrived = arrived.reshape((count_states,) + states[0].shape)
    return tuple((arrived[index] for index in range(count_states)))


def routed_gradient(tokens, cotangent, dest_ids, gate_probs, up_full):
    group_size = lax.axis_size("expert")
    tok_rows, top_count = dest_ids.shape
    width = tokens.shape[1]
    capacity = 3 * tok_rows * top_count // (2 * group_size)
    total = tok_rows * top_count
    flat_ids = dest_ids.reshape(-1)
    picked = (flat_ids[:, None] == jnp.arange(group_size, dtype=jnp.int32)[None, :]).astype(
        jnp.int32
    )
    ranking = jnp.sum((jnp.cumsum(picked, axis=0) - 1) * picked, axis=1)
    slot_index = flat_ids * capacity + ranking
    source = (
        jnp.full((group_size * capacity,), total, jnp.int32)
        .at[slot_index]
        .set(jnp.arange(total, dtype=jnp.int32))
    )
    filled = source < total
    safe_source = jnp.minimum(source, total - 1)
    row_index = safe_source // top_count
    weights_row = jnp.where(filled, gate_probs.reshape(-1)[safe_source], jnp.float32(0.0))
    sent_tokens = jnp.where(filled[:, None], tokens[row_index], jnp.zeros((), jnp.bfloat16))
    sent_scaled = (weights_row[:, None] * cotangent[row_index].astype(jnp.float32)).astype(
        jnp.bfloat16
    )
    sent_tokens = sent_tokens.reshape(group_size, capacity, width)
    sent_scaled = sent_scaled.reshape(group_size, capacity, width)
    got_tokens, got_scaled = (
        lax.all_to_all(sent_tokens, "expert", split_axis=0, concat_axis=0, tiled=True),
        lax.all_to_all(sent_scaled, "expert", split_axis=0, concat_axis=0, tiled=True),
    )
    rows_tokens = got_tokens.reshape(-1, width)
    rows_scaled = got_scaled.reshape(-1, width)
    hidden = jax.nn.silu(
        jnp.dot(rows_tokens, up_full, preferred_element_type=jnp.float32)
    ).astype(jnp.bfloat16)
    return lax.dot_general(
        hidden, rows_scaled, (((0,), (0,)), ((), ())), preferred_element_type=jnp.float32
    )


def dense_gradient(tokens, cotangent, expert_ids, gate_probs, up_full, expert):
    all_tokens = lax.all_gather(tokens, "expert", axis=0, tiled=True)
    all_cot = lax.all_gather(cotangent, "expert", axis=0, tiled=True)
    all_ids = lax.all_gather(expert_ids, "expert", axis=0, tiled=True)
    all_gates = lax.all_gather(gate_probs, "expert", axis=0, tiled=True)
    weights_row = jnp.sum(jnp.where(all_ids == expert, all_gates, jnp.float32(0.0)), axis=1)
    scaled = (weights_row[:, None] * all_cot.astype(jnp.float32)).astype(jnp.bfloat16)
    hidden = jax.nn.silu(
        jnp.dot(all_tokens, up_full, preferred_element_type=jnp.float32)
    ).astype(jnp.bfloat16)
    return lax.dot_general(
        hidden, scaled, (((0,), (0,)), ((), ())), preferred_element_type=jnp.float32
    )


def lamb_step(weight, moment_one, moment_two, gradient):
    first = beta_one * moment_one + (1.0 - beta_one) * gradient
    second = beta_two * moment_two + (1.0 - beta_two) * gradient * gradient
    update = first / (jnp.sqrt(second) + epsilon)
    weight_sq, update_sq = lax.psum((jnp.sum(weight * weight), jnp.sum(update * update)), "dp")
    trust_ratio = jnp.sqrt(weight_sq) / (jnp.sqrt(update_sq) + epsilon)
    renewed = weight - learn_rate * trust_ratio * update
    return (renewed, first, second)


def local(
    tokens, cotangent, expert_ids, gate_probs, up_weight, down_weight, moment1, moment2, pair_match
):
    group_size = lax.axis_size("expert")
    partner = pair_match[lax.axis_index("expert")]
    weight, moment_one, moment_two = relocate((down_weight[0], moment1[0], moment2[0]), pair_match)
    (up_local,) = relocate((up_weight[0],), pair_match)
    up_full = lax.all_gather(up_local, "dp", axis=1, tiled=True)
    if group_size * tokens.shape[0] <= dense_rows_max:
        partial = dense_gradient(tokens, cotangent, expert_ids, gate_probs, up_full, partner)
    else:
        partial = routed_gradient(tokens, cotangent, pair_match[expert_ids], gate_probs, up_full)
    gradient = lax.psum_scatter(partial, "dp", scatter_dimension=0, tiled=True)
    renewed, first, second = lamb_step(weight, moment_one, moment_two, gradient)
    return (renewed[None], first[None], second[None])


def solution(mesh):
    in_specs = (
        P(("dp", "expert"), None),
        P(("dp", "expert"), None),
        P(("dp", "expert"), None),
        P(("dp", "expert"), None),
        P("expert", None, "dp"),
        P("expert", "dp", None),
        P("expert", "dp", None),
        P("expert", "dp", None),
        P(),
    )
    out_specs = (P("expert", "dp", None), P("expert", "dp", None), P("expert", "dp", None))
    return jax.shard_map(local, mesh=mesh, in_specs=in_specs, out_specs=out_specs, check_vma=False)
```

```python
import jax
import jax.numpy as jnp
from jax import lax
from jax.sharding import PartitionSpec as P

beta_one = 0.9
beta_two = 0.999
epsilon = 1e-06
learn_rate = 0.05

dense_rows_max = 2048


def relocate(state, pair_match):
    group_size = lax.axis_size("expert")
    pieces = state.reshape((group_size, -1) + state.shape[1:])
    spread = lax.all_to_all(pieces, "expert", split_axis=0, concat_axis=0, tiled=True)
    chosen = jnp.take(spread, pair_match, axis=0)
    arrived = lax.all_to_all(chosen, "expert", split_axis=0, concat_axis=0, tiled=True)
    return arrived.reshape(state.shape)


def routed_gradient(tokens, cotangent, dest_ids, gate_probs, up_full):
    group_size = lax.axis_size("expert")
    tok_rows, top_count = dest_ids.shape
    width = tokens.shape[1]
    capacity = 3 * tok_rows * top_count // (2 * group_size)
    total = tok_rows * top_count
    flat_ids = dest_ids.reshape(-1)
    picked = (flat_ids[:, None] == jnp.arange(group_size, dtype=jnp.int32)[None, :]).astype(
        jnp.int32
    )
    ranking = jnp.sum((jnp.cumsum(picked, axis=0) - 1) * picked, axis=1)
    slot_index = flat_ids * capacity + ranking
    source = (
        jnp.full((group_size * capacity,), total, jnp.int32)
        .at[slot_index]
        .set(jnp.arange(total, dtype=jnp.int32))
    )
    filled = source < total
    safe_source = jnp.minimum(source, total - 1)
    row_index = safe_source // top_count
    weights_row = jnp.where(filled, gate_probs.reshape(-1)[safe_source], jnp.float32(0.0))
    sent_tokens = jnp.where(filled[:, None], tokens[row_index], jnp.zeros((), jnp.bfloat16))
    sent_scaled = (weights_row[:, None] * cotangent[row_index].astype(jnp.float32)).astype(
        jnp.bfloat16
    )
    sent_tokens = sent_tokens.reshape(group_size, capacity, width)
    sent_scaled = sent_scaled.reshape(group_size, capacity, width)
    got_tokens, got_scaled = (
        lax.all_to_all(sent_tokens, "expert", split_axis=0, concat_axis=0, tiled=True),
        lax.all_to_all(sent_scaled, "expert", split_axis=0, concat_axis=0, tiled=True),
    )
    rows_tokens = got_tokens.reshape(-1, width)
    rows_scaled = got_scaled.reshape(-1, width)
    hidden = jax.nn.silu(
        jnp.dot(rows_tokens, up_full, preferred_element_type=jnp.float32)
    ).astype(jnp.bfloat16)
    return lax.dot_general(
        hidden, rows_scaled, (((0,), (0,)), ((), ())), preferred_element_type=jnp.float32
    )


def dense_gradient(tokens, cotangent, expert_ids, gate_probs, up_full, expert):
    top_count = expert_ids.shape[1]
    rows = lax.all_gather(jnp.stack((tokens, cotangent)), "expert", axis=1, tiled=True)
    routing = jnp.concatenate((gate_probs, expert_ids.astype(jnp.float32)), axis=1)
    routing = lax.all_gather(routing, "expert", axis=0, tiled=True)
    all_gates, all_ids = routing[:, :top_count], routing[:, top_count:]
    chosen = all_ids == expert.astype(jnp.float32)
    weights_row = jnp.sum(jnp.where(chosen, all_gates, jnp.float32(0.0)), axis=1)
    scaled = (weights_row[:, None] * rows[1].astype(jnp.float32)).astype(jnp.bfloat16)
    hidden = jax.nn.silu(
        jnp.dot(rows[0], up_full, preferred_element_type=jnp.float32)
    ).astype(jnp.bfloat16)
    return lax.dot_general(
        hidden, scaled, (((0,), (0,)), ((), ())), preferred_element_type=jnp.float32
    )


def lamb_step(weight, moment_one, moment_two, gradient):
    first = beta_one * moment_one + (1.0 - beta_one) * gradient
    second = beta_two * moment_two + (1.0 - beta_two) * gradient * gradient
    update = first / (jnp.sqrt(second) + epsilon)
    weight_sq, update_sq = lax.psum((jnp.sum(weight * weight), jnp.sum(update * update)), "dp")
    trust_ratio = jnp.sqrt(weight_sq) / (jnp.sqrt(update_sq) + epsilon)
    renewed = weight - learn_rate * trust_ratio * update
    return (renewed, first, second)


def local(
    tokens, cotangent, expert_ids, gate_probs, up_weight, down_weight, moment1, moment2, pair_match
):
    group_size = lax.axis_size("expert")
    partner = pair_match[lax.axis_index("expert")]
    up_local = relocate(up_weight[0], pair_match)
    weight = relocate(down_weight[0], pair_match)
    moment_one = relocate(moment1[0], pair_match)
    moment_two = relocate(moment2[0], pair_match)
    up_full = lax.all_gather(up_local, "dp", axis=1, tiled=True)
    if group_size * tokens.shape[0] <= dense_rows_max:
        partial = dense_gradient(tokens, cotangent, expert_ids, gate_probs, up_full, partner)
    else:
        partial = routed_gradient(tokens, cotangent, pair_match[expert_ids], gate_probs, up_full)
    gradient = lax.psum_scatter(partial, "dp", scatter_dimension=0, tiled=True)
    renewed, first, second = lamb_step(weight, moment_one, moment_two, gradient)
    return (renewed[None], first[None], second[None])


def solution(mesh):
    in_specs = (
        P(("dp", "expert"), None),
        P(("dp", "expert"), None),
        P(("dp", "expert"), None),
        P(("dp", "expert"), None),
        P("expert", None, "dp"),
        P("expert", "dp", None),
        P("expert", "dp", None),
        P("expert", "dp", None),
        P(),
    )
    out_specs = (P("expert", "dp", None), P("expert", "dp", None), P("expert", "dp", None))
    return jax.shard_map(local, mesh=mesh, in_specs=in_specs, out_specs=out_specs, check_vma=False)
```

```python
import jax
import jax.numpy as jnp
from jax import lax
from jax.sharding import PartitionSpec as P

beta_one = 0.9
beta_two = 0.999
epsilon = 1e-06
learn_rate = 0.05

dense_rows_max = 2048
exchange_group_max = 8


def relocate(state, pair_match):
    group_size = lax.axis_size("expert")
    pieces = state.reshape((group_size, -1) + state.shape[1:])
    spread = lax.all_to_all(pieces, "expert", split_axis=0, concat_axis=0, tiled=True)
    chosen = jnp.take(spread, pair_match, axis=0)
    arrived = lax.all_to_all(chosen, "expert", split_axis=0, concat_axis=0, tiled=True)
    return arrived.reshape(state.shape)


def perfect_matchings(members):
    if not members:
        return [()]
    first, rest = members[0], members[1:]
    found = []
    for at, other in enumerate(rest):
        for tail in perfect_matchings(rest[:at] + rest[at + 1 :]):
            found.append(((first, other),) + tail)
    return found


def exchange(states, pair_match):
    group_size = lax.axis_size("expert")
    matchings = perfect_matchings(tuple(range(group_size)))
    scale = [group_size**place for place in range(group_size)]
    keys = [sum(scale[a] * b + scale[b] * a for a, b in pairs) for pairs in matchings]
    key = jnp.sum(pair_match * jnp.array(scale, jnp.int32))
    branch = jnp.argmax(jnp.array(keys, jnp.int32) == key).astype(jnp.int32)

    def swap(pairs):
        perm = [(a, b) for a, b in pairs] + [(b, a) for a, b in pairs]
        return lambda values: tuple(lax.ppermute(value, "expert", perm) for value in values)

    return lax.switch(branch, [swap(pairs) for pairs in matchings], tuple(states))


def routed_gradient(tokens, cotangent, dest_ids, gate_probs, up_full):
    group_size = lax.axis_size("expert")
    tok_rows, top_count = dest_ids.shape
    width = tokens.shape[1]
    capacity = 3 * tok_rows * top_count // (2 * group_size)
    total = tok_rows * top_count
    flat_ids = dest_ids.reshape(-1)
    picked = (flat_ids[:, None] == jnp.arange(group_size, dtype=jnp.int32)[None, :]).astype(
        jnp.int32
    )
    ranking = jnp.sum((jnp.cumsum(picked, axis=0) - 1) * picked, axis=1)
    slot_index = flat_ids * capacity + ranking
    source = (
        jnp.full((group_size * capacity,), total, jnp.int32)
        .at[slot_index]
        .set(jnp.arange(total, dtype=jnp.int32))
    )
    filled = source < total
    safe_source = jnp.minimum(source, total - 1)
    row_index = safe_source // top_count
    weights_row = jnp.where(filled, gate_probs.reshape(-1)[safe_source], jnp.float32(0.0))
    sent_tokens = jnp.where(filled[:, None], tokens[row_index], jnp.zeros((), jnp.bfloat16))
    sent_scaled = (weights_row[:, None] * cotangent[row_index].astype(jnp.float32)).astype(
        jnp.bfloat16
    )
    sent_tokens = sent_tokens.reshape(group_size, capacity, width)
    sent_scaled = sent_scaled.reshape(group_size, capacity, width)
    got_tokens, got_scaled = (
        lax.all_to_all(sent_tokens, "expert", split_axis=0, concat_axis=0, tiled=True),
        lax.all_to_all(sent_scaled, "expert", split_axis=0, concat_axis=0, tiled=True),
    )
    rows_tokens = got_tokens.reshape(-1, width)
    rows_scaled = got_scaled.reshape(-1, width)
    hidden = jax.nn.silu(
        jnp.dot(rows_tokens, up_full, preferred_element_type=jnp.float32)
    ).astype(jnp.bfloat16)
    return lax.dot_general(
        hidden, rows_scaled, (((0,), (0,)), ((), ())), preferred_element_type=jnp.float32
    )


def dense_gradient(tokens, cotangent, expert_ids, gate_probs, up_full, expert):
    top_count = expert_ids.shape[1]
    rows = lax.all_gather(jnp.stack((tokens, cotangent)), "expert", axis=1, tiled=True)
    routing = jnp.concatenate((gate_probs, expert_ids.astype(jnp.float32)), axis=1)
    routing = lax.all_gather(routing, "expert", axis=0, tiled=True)
    all_gates, all_ids = routing[:, :top_count], routing[:, top_count:]
    chosen = all_ids == expert.astype(jnp.float32)
    weights_row = jnp.sum(jnp.where(chosen, all_gates, jnp.float32(0.0)), axis=1)
    scaled = (weights_row[:, None] * rows[1].astype(jnp.float32)).astype(jnp.bfloat16)
    hidden = jax.nn.silu(
        jnp.dot(rows[0], up_full, preferred_element_type=jnp.float32)
    ).astype(jnp.bfloat16)
    return lax.dot_general(
        hidden, scaled, (((0,), (0,)), ((), ())), preferred_element_type=jnp.float32
    )


def lamb_step(weight, moment_one, moment_two, gradient):
    first = beta_one * moment_one + (1.0 - beta_one) * gradient
    second = beta_two * moment_two + (1.0 - beta_two) * gradient * gradient
    update = first / (jnp.sqrt(second) + epsilon)
    weight_sq, update_sq = lax.psum((jnp.sum(weight * weight), jnp.sum(update * update)), "dp")
    trust_ratio = jnp.sqrt(weight_sq) / (jnp.sqrt(update_sq) + epsilon)
    renewed = weight - learn_rate * trust_ratio * update
    return (renewed, first, second)


def local(
    tokens, cotangent, expert_ids, gate_probs, up_weight, down_weight, moment1, moment2, pair_match
):
    group_size = lax.axis_size("expert")
    partner = pair_match[lax.axis_index("expert")]
    states = (up_weight[0], down_weight[0], moment1[0], moment2[0])
    if group_size <= exchange_group_max:
        up_local, weight, moment_one, moment_two = exchange(states, pair_match)
    else:
        up_local, weight, moment_one, moment_two = (relocate(x, pair_match) for x in states)
    up_full = lax.all_gather(up_local, "dp", axis=1, tiled=True)
    if group_size * tokens.shape[0] <= dense_rows_max:
        partial = dense_gradient(tokens, cotangent, expert_ids, gate_probs, up_full, partner)
    else:
        partial = routed_gradient(tokens, cotangent, pair_match[expert_ids], gate_probs, up_full)
    gradient = lax.psum_scatter(partial, "dp", scatter_dimension=0, tiled=True)
    renewed, first, second = lamb_step(weight, moment_one, moment_two, gradient)
    return (renewed[None], first[None], second[None])


def solution(mesh):
    in_specs = (
        P(("dp", "expert"), None),
        P(("dp", "expert"), None),
        P(("dp", "expert"), None),
        P(("dp", "expert"), None),
        P("expert", None, "dp"),
        P("expert", "dp", None),
        P("expert", "dp", None),
        P("expert", "dp", None),
        P(),
    )
    out_specs = (P("expert", "dp", None), P("expert", "dp", None), P("expert", "dp", None))
    return jax.shard_map(local, mesh=mesh, in_specs=in_specs, out_specs=out_specs, check_vma=False)
```

```python
import jax
import jax.numpy as jnp
from jax import lax
from jax.sharding import PartitionSpec as P

beta_one = 0.9
beta_two = 0.999
epsilon = 1e-06
learn_rate = 0.05

dense_rows_max = 2048
exchange_group_max = 8


def relocate(state, pair_match):
    group_size = lax.axis_size("expert")
    pieces = state.reshape((group_size, -1) + state.shape[1:])
    spread = lax.all_to_all(pieces, "expert", split_axis=0, concat_axis=0, tiled=True)
    chosen = jnp.take(spread, pair_match, axis=0)
    arrived = lax.all_to_all(chosen, "expert", split_axis=0, concat_axis=0, tiled=True)
    return arrived.reshape(state.shape)


def perfect_matchings(members):
    if not members:
        return [()]
    first, rest = members[0], members[1:]
    found = []
    for at, other in enumerate(rest):
        for tail in perfect_matchings(rest[:at] + rest[at + 1 :]):
            found.append(((first, other),) + tail)
    return found


def exchange(states, pair_match):
    group_size = lax.axis_size("expert")
    matchings = perfect_matchings(tuple(range(group_size)))
    scale = [group_size**place for place in range(group_size)]
    keys = [sum(scale[a] * b + scale[b] * a for a, b in pairs) for pairs in matchings]
    key = jnp.sum(pair_match * jnp.array(scale, jnp.int32))
    branch = jnp.argmax(jnp.array(keys, jnp.int32) == key).astype(jnp.int32)

    def swap(pairs):
        perm = [(a, b) for a, b in pairs] + [(b, a) for a, b in pairs]
        return lambda values: tuple(lax.ppermute(value, "expert", perm) for value in values)

    return lax.switch(branch, [swap(pairs) for pairs in matchings], tuple(states))


def routed_gradient(tokens, cotangent, dest_ids, gate_probs, up_full):
    group_size = lax.axis_size("expert")
    tok_rows, top_count = dest_ids.shape
    width = tokens.shape[1]
    capacity = 3 * tok_rows * top_count // (2 * group_size)
    total = tok_rows * top_count
    flat_ids = dest_ids.reshape(-1)
    picked = (flat_ids[:, None] == jnp.arange(group_size, dtype=jnp.int32)[None, :]).astype(
        jnp.int32
    )
    ranking = jnp.sum((jnp.cumsum(picked, axis=0) - 1) * picked, axis=1)
    slot_index = flat_ids * capacity + ranking
    source = (
        jnp.full((group_size * capacity,), total, jnp.int32)
        .at[slot_index]
        .set(jnp.arange(total, dtype=jnp.int32))
    )
    filled = source < total
    safe_source = jnp.minimum(source, total - 1)
    row_index = safe_source // top_count
    weights_row = jnp.where(filled, gate_probs.reshape(-1)[safe_source], jnp.float32(0.0))
    sent_tokens = jnp.where(filled[:, None], tokens[row_index], jnp.zeros((), jnp.bfloat16))
    sent_scaled = (weights_row[:, None] * cotangent[row_index].astype(jnp.float32)).astype(
        jnp.bfloat16
    )
    sent_tokens = sent_tokens.reshape(group_size, capacity, width)
    sent_scaled = sent_scaled.reshape(group_size, capacity, width)
    got_tokens, got_scaled = (
        lax.all_to_all(sent_tokens, "expert", split_axis=0, concat_axis=0, tiled=True),
        lax.all_to_all(sent_scaled, "expert", split_axis=0, concat_axis=0, tiled=True),
    )
    rows_tokens = got_tokens.reshape(-1, width)
    rows_scaled = got_scaled.reshape(-1, width)
    hidden = jax.nn.silu(
        jnp.dot(rows_tokens, up_full, preferred_element_type=jnp.float32)
    ).astype(jnp.bfloat16)
    return lax.dot_general(
        hidden, rows_scaled, (((0,), (0,)), ((), ())), preferred_element_type=jnp.float32
    )


def dense_gradient(tokens, cotangent, expert_ids, gate_probs, up_local, expert):
    top_count = expert_ids.shape[1]
    rows = lax.all_gather(jnp.stack((tokens, cotangent)), "expert", axis=1, tiled=True)
    rows, up_local = lax.optimization_barrier((rows, up_local))
    up_full = lax.all_gather(up_local, "dp", axis=1, tiled=True)
    routing = jnp.concatenate((gate_probs, expert_ids.astype(jnp.float32)), axis=1)
    routing = lax.all_gather(routing, "expert", axis=0, tiled=True)
    all_gates, all_ids = routing[:, :top_count], routing[:, top_count:]
    chosen = all_ids == expert.astype(jnp.float32)
    weights_row = jnp.sum(jnp.where(chosen, all_gates, jnp.float32(0.0)), axis=1)
    scaled = (weights_row[:, None] * rows[1].astype(jnp.float32)).astype(jnp.bfloat16)
    hidden = jax.nn.silu(
        jnp.dot(rows[0], up_full, preferred_element_type=jnp.float32)
    ).astype(jnp.bfloat16)
    return lax.dot_general(
        hidden, scaled, (((0,), (0,)), ((), ())), preferred_element_type=jnp.float32
    )


def lamb_step(weight, moment_one, moment_two, gradient):
    first = beta_one * moment_one + (1.0 - beta_one) * gradient
    second = beta_two * moment_two + (1.0 - beta_two) * gradient * gradient
    update = first / (jnp.sqrt(second) + epsilon)
    weight_sq, update_sq = lax.psum((jnp.sum(weight * weight), jnp.sum(update * update)), "dp")
    trust_ratio = jnp.sqrt(weight_sq) / (jnp.sqrt(update_sq) + epsilon)
    renewed = weight - learn_rate * trust_ratio * update
    return (renewed, first, second)


def local(
    tokens, cotangent, expert_ids, gate_probs, up_weight, down_weight, moment1, moment2, pair_match
):
    group_size = lax.axis_size("expert")
    partner = pair_match[lax.axis_index("expert")]
    states = (down_weight[0], moment1[0], moment2[0])
    if group_size <= exchange_group_max:
        up_wide = up_weight[0].astype(jnp.float32).reshape(states[0].shape)
        (swapped,) = exchange((jnp.stack((up_wide,) + states),), pair_match)
        up_local = swapped[0].reshape(up_weight.shape[1:]).astype(jnp.bfloat16)
        weight, moment_one, moment_two = swapped[1], swapped[2], swapped[3]
    else:
        up_local = relocate(up_weight[0], pair_match)
        weight, moment_one, moment_two = (relocate(x, pair_match) for x in states)
    if group_size * tokens.shape[0] <= dense_rows_max:
        partial = dense_gradient(tokens, cotangent, expert_ids, gate_probs, up_local, partner)
    else:
        up_full = lax.all_gather(up_local, "dp", axis=1, tiled=True)
        partial = routed_gradient(tokens, cotangent, pair_match[expert_ids], gate_probs, up_full)
    gradient = lax.psum_scatter(partial, "dp", scatter_dimension=0, tiled=True)
    renewed, first, second = lamb_step(weight, moment_one, moment_two, gradient)
    return (renewed[None], first[None], second[None])


def solution(mesh):
    in_specs = (
        P(("dp", "expert"), None),
        P(("dp", "expert"), None),
        P(("dp", "expert"), None),
        P(("dp", "expert"), None),
        P("expert", None, "dp"),
        P("expert", "dp", None),
        P("expert", "dp", None),
        P("expert", "dp", None),
        P(),
    )
    out_specs = (P("expert", "dp", None), P("expert", "dp", None), P("expert", "dp", None))
    return jax.shard_map(local, mesh=mesh, in_specs=in_specs, out_specs=out_specs, check_vma=False)
```

```python
import jax
import jax.numpy as jnp
from jax import lax
from jax.sharding import PartitionSpec as P

beta_one = 0.9
beta_two = 0.999
epsilon = 1e-06
learn_rate = 0.05

dense_rows_max = 2048
exchange_group_max = 8


def relocate(state, pair_match):
    group_size = lax.axis_size("expert")
    pieces = state.reshape((group_size, -1) + state.shape[1:])
    spread = lax.all_to_all(pieces, "expert", split_axis=0, concat_axis=0, tiled=True)
    chosen = jnp.take(spread, pair_match, axis=0)
    arrived = lax.all_to_all(chosen, "expert", split_axis=0, concat_axis=0, tiled=True)
    return arrived.reshape(state.shape)


def perfect_matchings(members):
    if not members:
        return [()]
    first, rest = members[0], members[1:]
    found = []
    for at, other in enumerate(rest):
        for tail in perfect_matchings(rest[:at] + rest[at + 1 :]):
            found.append(((first, other),) + tail)
    return found


def exchange(states, pair_match):
    group_size = lax.axis_size("expert")
    matchings = perfect_matchings(tuple(range(group_size)))
    scale = [group_size**place for place in range(group_size)]
    keys = [sum(scale[a] * b + scale[b] * a for a, b in pairs) for pairs in matchings]
    key = jnp.sum(pair_match * jnp.array(scale, jnp.int32))
    branch = jnp.argmax(jnp.array(keys, jnp.int32) == key).astype(jnp.int32)

    def swap(pairs):
        perm = [(a, b) for a, b in pairs] + [(b, a) for a, b in pairs]
        return lambda values: tuple(lax.ppermute(value, "expert", perm) for value in values)

    return lax.switch(branch, [swap(pairs) for pairs in matchings], tuple(states))


def routed_gradient(tokens, cotangent, dest_ids, gate_probs, up_full):
    group_size = lax.axis_size("expert")
    tok_rows, top_count = dest_ids.shape
    width = tokens.shape[1]
    capacity = 3 * tok_rows * top_count // (2 * group_size)
    total = tok_rows * top_count
    flat_ids = dest_ids.reshape(-1)
    picked = (flat_ids[:, None] == jnp.arange(group_size, dtype=jnp.int32)[None, :]).astype(
        jnp.int32
    )
    ranking = jnp.sum((jnp.cumsum(picked, axis=0) - 1) * picked, axis=1)
    slot_index = flat_ids * capacity + ranking
    source = (
        jnp.full((group_size * capacity,), total, jnp.int32)
        .at[slot_index]
        .set(jnp.arange(total, dtype=jnp.int32))
    )
    filled = source < total
    safe_source = jnp.minimum(source, total - 1)
    row_index = safe_source // top_count
    weights_row = jnp.where(filled, gate_probs.reshape(-1)[safe_source], jnp.float32(0.0))
    sent_tokens = jnp.where(filled[:, None], tokens[row_index], jnp.zeros((), jnp.bfloat16))
    sent_scaled = (weights_row[:, None] * cotangent[row_index].astype(jnp.float32)).astype(
        jnp.bfloat16
    )
    sent_tokens = sent_tokens.reshape(group_size, capacity, width)
    sent_scaled = sent_scaled.reshape(group_size, capacity, width)
    got_tokens, got_scaled = (
        lax.all_to_all(sent_tokens, "expert", split_axis=0, concat_axis=0, tiled=True),
        lax.all_to_all(sent_scaled, "expert", split_axis=0, concat_axis=0, tiled=True),
    )
    rows_tokens = got_tokens.reshape(-1, width)
    rows_scaled = got_scaled.reshape(-1, width)
    hidden = jax.nn.silu(
        jnp.dot(rows_tokens, up_full, preferred_element_type=jnp.float32)
    ).astype(jnp.bfloat16)
    return lax.dot_general(
        hidden, rows_scaled, (((0,), (0,)), ((), ())), preferred_element_type=jnp.float32
    )


def dense_gradient(tokens, cotangent, expert_ids, gate_probs, up_local, expert):
    top_count = expert_ids.shape[1]
    rows = lax.all_gather(jnp.stack((tokens, cotangent)), "expert", axis=1, tiled=True)
    rows, up_local = lax.optimization_barrier((rows, up_local))
    up_full = lax.all_gather(up_local, "dp", axis=1, tiled=True)
    routing = jnp.concatenate((gate_probs, expert_ids.astype(jnp.float32)), axis=1)
    routing = lax.all_gather(routing, "expert", axis=0, tiled=True)
    all_gates, all_ids = routing[:, :top_count], routing[:, top_count:]
    chosen = all_ids == expert.astype(jnp.float32)
    weights_row = jnp.sum(jnp.where(chosen, all_gates, jnp.float32(0.0)), axis=1)
    scaled = (weights_row[:, None] * rows[1].astype(jnp.float32)).astype(jnp.bfloat16)
    hidden = jax.nn.silu(
        jnp.dot(rows[0], up_full, preferred_element_type=jnp.float32)
    ).astype(jnp.bfloat16)
    middle = scaled.shape[1] // 2
    return tuple(
        lax.dot_general(
            hidden, part, (((0,), (0,)), ((), ())), preferred_element_type=jnp.float32
        )
        for part in (scaled[:, :middle], scaled[:, middle:])
    )


def grid_reduce_scatter(halves):
    where = lax.axis_index("dp")
    low, high = where % 2, where // 2
    size = lax.axis_size("dp")
    flip_low = [(d, d ^ 1) for d in range(size)]
    flip_high = [(d, d ^ 2) for d in range(size)]
    first, second = (half.reshape((2, 2, -1) + half.shape[1:]) for half in halves)
    sent = lax.ppermute(jnp.take(first, 1 - low, axis=1), "dp", flip_low)
    first = jnp.take(first, low, axis=1) + sent
    sent = lax.ppermute(jnp.take(second, 1 - high, axis=0), "dp", flip_high)
    second = jnp.take(second, high, axis=0) + sent
    sent = lax.ppermute(jnp.take(first, 1 - high, axis=0), "dp", flip_high)
    first = jnp.take(first, high, axis=0) + sent
    sent = lax.ppermute(jnp.take(second, 1 - low, axis=0), "dp", flip_low)
    second = jnp.take(second, low, axis=0) + sent
    return jnp.concatenate((first, second), axis=1)


def lamb_step(weight, moment_one, moment_two, gradient):
    first = beta_one * moment_one + (1.0 - beta_one) * gradient
    second = beta_two * moment_two + (1.0 - beta_two) * gradient * gradient
    update = first / (jnp.sqrt(second) + epsilon)
    weight_sq, update_sq = lax.psum((jnp.sum(weight * weight), jnp.sum(update * update)), "dp")
    trust_ratio = jnp.sqrt(weight_sq) / (jnp.sqrt(update_sq) + epsilon)
    renewed = weight - learn_rate * trust_ratio * update
    return (renewed, first, second)


def local(
    tokens, cotangent, expert_ids, gate_probs, up_weight, down_weight, moment1, moment2, pair_match
):
    group_size = lax.axis_size("expert")
    partner = pair_match[lax.axis_index("expert")]
    states = (down_weight[0], moment1[0], moment2[0])
    if group_size <= exchange_group_max:
        up_wide = up_weight[0].astype(jnp.float32).reshape(states[0].shape)
        (swapped,) = exchange((jnp.stack((up_wide,) + states),), pair_match)
        up_local = swapped[0].reshape(up_weight.shape[1:]).astype(jnp.bfloat16)
        weight, moment_one, moment_two = swapped[1], swapped[2], swapped[3]
    else:
        up_local = relocate(up_weight[0], pair_match)
        weight, moment_one, moment_two = (relocate(x, pair_match) for x in states)
    if group_size * tokens.shape[0] <= dense_rows_max:
        halves = dense_gradient(tokens, cotangent, expert_ids, gate_probs, up_local, partner)
    else:
        up_full = lax.all_gather(up_local, "dp", axis=1, tiled=True)
        partial = routed_gradient(tokens, cotangent, pair_match[expert_ids], gate_probs, up_full)
        middle = partial.shape[1] // 2
        halves = (partial[:, :middle], partial[:, middle:])
    if lax.axis_size("dp") == 4 and halves[0].shape[0] % 4 == 0:
        gradient = grid_reduce_scatter(halves)
    else:
        gradient = lax.psum_scatter(
            jnp.concatenate(halves, axis=1), "dp", scatter_dimension=0, tiled=True
        )
    renewed, first, second = lamb_step(weight, moment_one, moment_two, gradient)
    return (renewed[None], first[None], second[None])


def solution(mesh):
    in_specs = (
        P(("dp", "expert"), None),
        P(("dp", "expert"), None),
        P(("dp", "expert"), None),
        P(("dp", "expert"), None),
        P("expert", None, "dp"),
        P("expert", "dp", None),
        P("expert", "dp", None),
        P("expert", "dp", None),
        P(),
    )
    out_specs = (P("expert", "dp", None), P("expert", "dp", None), P("expert", "dp", None))
    return jax.shard_map(local, mesh=mesh, in_specs=in_specs, out_specs=out_specs, check_vma=False)
```

```python
import jax
import jax.numpy as jnp
from jax import lax
from jax.sharding import PartitionSpec as P

beta_one = 0.9
beta_two = 0.999
epsilon = 1e-06
learn_rate = 0.05

dense_rows_max = 2048
exchange_group_max = 8


def relocate(state, pair_match):
    group_size = lax.axis_size("expert")
    pieces = state.reshape((group_size, -1) + state.shape[1:])
    spread = lax.all_to_all(pieces, "expert", split_axis=0, concat_axis=0, tiled=True)
    chosen = jnp.take(spread, pair_match, axis=0)
    arrived = lax.all_to_all(chosen, "expert", split_axis=0, concat_axis=0, tiled=True)
    return arrived.reshape(state.shape)


def perfect_matchings(members):
    if not members:
        return [()]
    first, rest = members[0], members[1:]
    found = []
    for at, other in enumerate(rest):
        for tail in perfect_matchings(rest[:at] + rest[at + 1 :]):
            found.append(((first, other),) + tail)
    return found


def exchange(states, pair_match):
    group_size = lax.axis_size("expert")
    matchings = perfect_matchings(tuple(range(group_size)))
    scale = [group_size**place for place in range(group_size)]
    keys = [sum(scale[a] * b + scale[b] * a for a, b in pairs) for pairs in matchings]
    key = jnp.sum(pair_match * jnp.array(scale, jnp.int32))
    branch = jnp.argmax(jnp.array(keys, jnp.int32) == key).astype(jnp.int32)

    def swap(pairs):
        perm = [(a, b) for a, b in pairs] + [(b, a) for a, b in pairs]
        return lambda values: tuple(lax.ppermute(value, "expert", perm) for value in values)

    return lax.switch(branch, [swap(pairs) for pairs in matchings], tuple(states))


def routed_gradient(tokens, cotangent, dest_ids, gate_probs, up_full):
    group_size = lax.axis_size("expert")
    tok_rows, top_count = dest_ids.shape
    width = tokens.shape[1]
    capacity = 3 * tok_rows * top_count // (2 * group_size)
    total = tok_rows * top_count
    flat_ids = dest_ids.reshape(-1)
    picked = (flat_ids[:, None] == jnp.arange(group_size, dtype=jnp.int32)[None, :]).astype(
        jnp.int32
    )
    ranking = jnp.sum((jnp.cumsum(picked, axis=0) - 1) * picked, axis=1)
    slot_index = flat_ids * capacity + ranking
    source = (
        jnp.full((group_size * capacity,), total, jnp.int32)
        .at[slot_index]
        .set(jnp.arange(total, dtype=jnp.int32))
    )
    filled = source < total
    safe_source = jnp.minimum(source, total - 1)
    row_index = safe_source // top_count
    weights_row = jnp.where(filled, gate_probs.reshape(-1)[safe_source], jnp.float32(0.0))
    sent_tokens = jnp.where(filled[:, None], tokens[row_index], jnp.zeros((), jnp.bfloat16))
    sent_scaled = (weights_row[:, None] * cotangent[row_index].astype(jnp.float32)).astype(
        jnp.bfloat16
    )
    sent_tokens = sent_tokens.reshape(group_size, capacity, width)
    sent_scaled = sent_scaled.reshape(group_size, capacity, width)
    got_tokens, got_scaled = (
        lax.all_to_all(sent_tokens, "expert", split_axis=0, concat_axis=0, tiled=True),
        lax.all_to_all(sent_scaled, "expert", split_axis=0, concat_axis=0, tiled=True),
    )
    rows_tokens = got_tokens.reshape(-1, width)
    rows_scaled = got_scaled.reshape(-1, width)
    hidden = jax.nn.silu(
        jnp.dot(rows_tokens, up_full, preferred_element_type=jnp.float32)
    ).astype(jnp.bfloat16)
    return lax.dot_general(
        hidden, rows_scaled, (((0,), (0,)), ((), ())), preferred_element_type=jnp.float32
    )


def dense_gradient(tokens, cotangent, expert_ids, gate_probs, up_local, expert):
    top_count = expert_ids.shape[1]
    rows = lax.all_gather(jnp.stack((tokens, cotangent)), "expert", axis=1, tiled=True)
    rows, up_local = lax.optimization_barrier((rows, up_local))
    up_full = lax.all_gather(up_local, "dp", axis=1, tiled=True)
    routing = jnp.concatenate((gate_probs, expert_ids.astype(jnp.float32)), axis=1)
    routing = lax.all_gather(routing, "expert", axis=0, tiled=True)
    all_gates, all_ids = routing[:, :top_count], routing[:, top_count:]
    chosen = all_ids == expert.astype(jnp.float32)
    weights_row = jnp.sum(jnp.where(chosen, all_gates, jnp.float32(0.0)), axis=1)
    scaled = (weights_row[:, None] * rows[1].astype(jnp.float32)).astype(jnp.bfloat16)
    hidden = jax.nn.silu(
        jnp.dot(rows[0], up_full, preferred_element_type=jnp.float32)
    ).astype(jnp.bfloat16)
    middle = scaled.shape[1] // 2
    return tuple(
        lax.dot_general(
            hidden, part, (((0,), (0,)), ((), ())), preferred_element_type=jnp.float32
        )
        for part in (scaled[:, :middle], scaled[:, middle:])
    )


def grid_reduce_scatter(halves):
    where = lax.axis_index("dp")
    low, high = where % 2, where // 2
    size = lax.axis_size("dp")
    flip_low = [(d, d ^ 1) for d in range(size)]
    flip_high = [(d, d ^ 2) for d in range(size)]
    first, second = (half.reshape((2, 2, -1) + half.shape[1:]) for half in halves)
    sent = lax.ppermute(jnp.take(first, 1 - low, axis=1), "dp", flip_low)
    first = jnp.take(first, low, axis=1) + sent
    sent = lax.ppermute(jnp.take(second, 1 - high, axis=0), "dp", flip_high)
    second = jnp.take(second, high, axis=0) + sent
    sent = lax.ppermute(jnp.take(first, 1 - high, axis=0), "dp", flip_high)
    first = jnp.take(first, high, axis=0) + sent
    sent = lax.ppermute(jnp.take(second, 1 - low, axis=0), "dp", flip_low)
    second = jnp.take(second, low, axis=0) + sent
    return jnp.concatenate((first, second), axis=1)


def lamb_step(weight, moment_one, moment_two, gradient):
    first = beta_one * moment_one + (1.0 - beta_one) * gradient
    second = beta_two * moment_two + (1.0 - beta_two) * gradient * gradient
    update = first / (jnp.sqrt(second) + epsilon)
    weight_sq, update_sq = lax.psum((jnp.sum(weight * weight), jnp.sum(update * update)), "dp")
    trust_ratio = jnp.sqrt(weight_sq) / (jnp.sqrt(update_sq) + epsilon)
    renewed = weight - learn_rate * trust_ratio * update
    return (renewed, first, second)


def local(
    tokens, cotangent, expert_ids, gate_probs, up_weight, down_weight, moment1, moment2, pair_match
):
    group_size = lax.axis_size("expert")
    partner = pair_match[lax.axis_index("expert")]
    states = (down_weight[0], moment1[0], moment2[0])
    swap_direct = group_size <= exchange_group_max
    if swap_direct:
        (up_local,) = exchange((up_weight[0],), pair_match)
    else:
        up_local = relocate(up_weight[0], pair_match)
    if group_size * tokens.shape[0] <= dense_rows_max:
        halves = dense_gradient(tokens, cotangent, expert_ids, gate_probs, up_local, partner)
    else:
        up_full = lax.all_gather(up_local, "dp", axis=1, tiled=True)
        partial = routed_gradient(tokens, cotangent, pair_match[expert_ids], gate_probs, up_full)
        middle = partial.shape[1] // 2
        halves = (partial[:, :middle], partial[:, middle:])
    if swap_direct:
        states, halves = lax.optimization_barrier((states, halves))
        (swapped,) = exchange((jnp.stack(states),), pair_match)
        weight, moment_one, moment_two = swapped[0], swapped[1], swapped[2]
        gradient = lax.psum_scatter(
            jnp.concatenate(halves, axis=1), "dp", scatter_dimension=0, tiled=True
        )
    else:
        weight, moment_one, moment_two = (relocate(x, pair_match) for x in states)
        if lax.axis_size("dp") == 4 and halves[0].shape[0] % 4 == 0:
            gradient = grid_reduce_scatter(halves)
        else:
            gradient = lax.psum_scatter(
                jnp.concatenate(halves, axis=1), "dp", scatter_dimension=0, tiled=True
            )
    renewed, first, second = lamb_step(weight, moment_one, moment_two, gradient)
    return (renewed[None], first[None], second[None])


def solution(mesh):
    in_specs = (
        P(("dp", "expert"), None),
        P(("dp", "expert"), None),
        P(("dp", "expert"), None),
        P(("dp", "expert"), None),
        P("expert", None, "dp"),
        P("expert", "dp", None),
        P("expert", "dp", None),
        P("expert", "dp", None),
        P(),
    )
    out_specs = (P("expert", "dp", None), P("expert", "dp", None), P("expert", "dp", None))
    return jax.shard_map(local, mesh=mesh, in_specs=in_specs, out_specs=out_specs, check_vma=False)
```

```python
import jax
import jax.numpy as jnp
from jax import lax
from jax.sharding import PartitionSpec as P

beta_one = 0.9
beta_two = 0.999
epsilon = 1e-06
learn_rate = 0.05

dense_rows_max = 2048
exchange_group_max = 8


def relocate(state, pair_match):
    group_size = lax.axis_size("expert")
    pieces = state.reshape((group_size, -1) + state.shape[1:])
    spread = lax.all_to_all(pieces, "expert", split_axis=0, concat_axis=0, tiled=True)
    chosen = jnp.take(spread, pair_match, axis=0)
    arrived = lax.all_to_all(chosen, "expert", split_axis=0, concat_axis=0, tiled=True)
    return arrived.reshape(state.shape)


def perfect_matchings(members):
    if not members:
        return [()]
    first, rest = members[0], members[1:]
    found = []
    for at, other in enumerate(rest):
        for tail in perfect_matchings(rest[:at] + rest[at + 1 :]):
            found.append(((first, other),) + tail)
    return found


def exchange(states, pair_match):
    group_size = lax.axis_size("expert")
    matchings = perfect_matchings(tuple(range(group_size)))
    scale = [group_size**place for place in range(group_size)]
    keys = [sum(scale[a] * b + scale[b] * a for a, b in pairs) for pairs in matchings]
    key = jnp.sum(pair_match * jnp.array(scale, jnp.int32))
    branch = jnp.argmax(jnp.array(keys, jnp.int32) == key).astype(jnp.int32)

    def swap(pairs):
        perm = [(a, b) for a, b in pairs] + [(b, a) for a, b in pairs]
        return lambda values: tuple(lax.ppermute(value, "expert", perm) for value in values)

    return lax.switch(branch, [swap(pairs) for pairs in matchings], tuple(states))


def routed_gradient(tokens, cotangent, dest_ids, gate_probs, up_full):
    group_size = lax.axis_size("expert")
    tok_rows, top_count = dest_ids.shape
    width = tokens.shape[1]
    capacity = 3 * tok_rows * top_count // (2 * group_size)
    total = tok_rows * top_count
    flat_ids = dest_ids.reshape(-1)
    picked = (flat_ids[:, None] == jnp.arange(group_size, dtype=jnp.int32)[None, :]).astype(
        jnp.int32
    )
    ranking = jnp.sum((jnp.cumsum(picked, axis=0) - 1) * picked, axis=1)
    slot_index = flat_ids * capacity + ranking
    source = (
        jnp.full((group_size * capacity,), total, jnp.int32)
        .at[slot_index]
        .set(jnp.arange(total, dtype=jnp.int32))
    )
    filled = source < total
    safe_source = jnp.minimum(source, total - 1)
    row_index = safe_source // top_count
    weights_row = jnp.where(filled, gate_probs.reshape(-1)[safe_source], jnp.float32(0.0))
    sent_tokens = jnp.where(filled[:, None], tokens[row_index], jnp.zeros((), jnp.bfloat16))
    sent_scaled = (weights_row[:, None] * cotangent[row_index].astype(jnp.float32)).astype(
        jnp.bfloat16
    )
    sent_tokens = sent_tokens.reshape(group_size, capacity, width)
    sent_scaled = sent_scaled.reshape(group_size, capacity, width)
    got_tokens, got_scaled = (
        lax.all_to_all(sent_tokens, "expert", split_axis=0, concat_axis=0, tiled=True),
        lax.all_to_all(sent_scaled, "expert", split_axis=0, concat_axis=0, tiled=True),
    )
    rows_tokens = got_tokens.reshape(-1, width)
    rows_scaled = got_scaled.reshape(-1, width)
    hidden = jax.nn.silu(
        jnp.dot(rows_tokens, up_full, preferred_element_type=jnp.float32)
    ).astype(jnp.bfloat16)
    return lax.dot_general(
        hidden, rows_scaled, (((0,), (0,)), ((), ())), preferred_element_type=jnp.float32
    )


def gather_group(tokens, cotangent, expert_ids, gate_probs):
    rows = lax.all_gather(jnp.stack((tokens, cotangent)), "expert", axis=1, tiled=True)
    routing = jnp.concatenate((gate_probs, expert_ids.astype(jnp.float32)), axis=1)
    routing = lax.all_gather(routing, "expert", axis=0, tiled=True)
    return rows, routing


def dense_gradient(rows, routing, up_full, expert):
    top_count = routing.shape[1] // 2
    all_gates, all_ids = routing[:, :top_count], routing[:, top_count:]
    chosen = all_ids == expert.astype(jnp.float32)
    weights_row = jnp.sum(jnp.where(chosen, all_gates, jnp.float32(0.0)), axis=1)
    scaled = (weights_row[:, None] * rows[1].astype(jnp.float32)).astype(jnp.bfloat16)
    hidden = jax.nn.silu(
        jnp.dot(rows[0], up_full, preferred_element_type=jnp.float32)
    ).astype(jnp.bfloat16)
    return lax.dot_general(
        hidden, scaled, (((0,), (0,)), ((), ())), preferred_element_type=jnp.float32
    )


def grid_reduce_scatter(halves):
    where = lax.axis_index("dp")
    low, high = where % 2, where // 2
    size = lax.axis_size("dp")
    flip_low = [(d, d ^ 1) for d in range(size)]
    flip_high = [(d, d ^ 2) for d in range(size)]
    first, second = (half.reshape((2, 2, -1) + half.shape[1:]) for half in halves)
    sent = lax.ppermute(jnp.take(first, 1 - low, axis=1), "dp", flip_low)
    first = jnp.take(first, low, axis=1) + sent
    sent = lax.ppermute(jnp.take(second, 1 - high, axis=0), "dp", flip_high)
    second = jnp.take(second, high, axis=0) + sent
    sent = lax.ppermute(jnp.take(first, 1 - high, axis=0), "dp", flip_high)
    first = jnp.take(first, high, axis=0) + sent
    sent = lax.ppermute(jnp.take(second, 1 - low, axis=0), "dp", flip_low)
    second = jnp.take(second, low, axis=0) + sent
    return jnp.concatenate((first, second), axis=1)


def lamb_step(weight, moment_one, moment_two, gradient):
    first = beta_one * moment_one + (1.0 - beta_one) * gradient
    second = beta_two * moment_two + (1.0 - beta_two) * gradient * gradient
    update = first / (jnp.sqrt(second) + epsilon)
    weight_sq, update_sq = lax.psum((jnp.sum(weight * weight), jnp.sum(update * update)), "dp")
    trust_ratio = jnp.sqrt(weight_sq) / (jnp.sqrt(update_sq) + epsilon)
    renewed = weight - learn_rate * trust_ratio * update
    return (renewed, first, second)


def local(
    tokens, cotangent, expert_ids, gate_probs, up_weight, down_weight, moment1, moment2, pair_match
):
    group_size = lax.axis_size("expert")
    partner = pair_match[lax.axis_index("expert")]
    if group_size <= exchange_group_max and group_size * tokens.shape[0] <= dense_rows_max:
        rows, routing = gather_group(tokens, cotangent, expert_ids, gate_probs)
        up_wide = up_weight[0].astype(jnp.float32).reshape(down_weight.shape[1:])
        routing, up_wide = lax.optimization_barrier((routing, up_wide))
        (swapped,) = exchange((jnp.stack((up_wide, down_weight[0])),), pair_match)
        up_local = swapped[0].reshape(up_weight.shape[1:]).astype(jnp.bfloat16)
        weight = swapped[1]
        rows, up_local = lax.optimization_barrier((rows, up_local))
        up_full = lax.all_gather(up_local, "dp", axis=1, tiled=True)
        partial = dense_gradient(rows, routing, up_full, partner)
        moments, partial = lax.optimization_barrier(((moment1[0], moment2[0]), partial))
        (swapped,) = exchange((jnp.stack(moments),), pair_match)
        moment_one, moment_two = swapped[0], swapped[1]
        gradient = lax.psum_scatter(partial, "dp", scatter_dimension=0, tiled=True)
    else:
        up_local = relocate(up_weight[0], pair_match)
        up_full = lax.all_gather(up_local, "dp", axis=1, tiled=True)
        partial = routed_gradient(tokens, cotangent, pair_match[expert_ids], gate_probs, up_full)
        weight, moment_one, moment_two = (
            relocate(x[0], pair_match) for x in (down_weight, moment1, moment2)
        )
        if lax.axis_size("dp") == 4 and partial.shape[0] % 4 == 0:
            middle = partial.shape[1] // 2
            gradient = grid_reduce_scatter((partial[:, :middle], partial[:, middle:]))
        else:
            gradient = lax.psum_scatter(partial, "dp", scatter_dimension=0, tiled=True)
    renewed, first, second = lamb_step(weight, moment_one, moment_two, gradient)
    return (renewed[None], first[None], second[None])


def solution(mesh):
    in_specs = (
        P(("dp", "expert"), None),
        P(("dp", "expert"), None),
        P(("dp", "expert"), None),
        P(("dp", "expert"), None),
        P("expert", None, "dp"),
        P("expert", "dp", None),
        P("expert", "dp", None),
        P("expert", "dp", None),
        P(),
    )
    out_specs = (P("expert", "dp", None), P("expert", "dp", None), P("expert", "dp", None))
    return jax.shard_map(local, mesh=mesh, in_specs=in_specs, out_specs=out_specs, check_vma=False)
```

```python
import jax
import jax.numpy as jnp
from jax import lax
from jax.sharding import PartitionSpec as P

beta_one = 0.9
beta_two = 0.999
epsilon = 1e-06
learn_rate = 0.05

dense_rows_max = 2048
exchange_group_max = 8


def relocate(state, pair_match):
    group_size = lax.axis_size("expert")
    pieces = state.reshape((group_size, -1) + state.shape[1:])
    spread = lax.all_to_all(pieces, "expert", split_axis=0, concat_axis=0, tiled=True)
    chosen = jnp.take(spread, pair_match, axis=0)
    arrived = lax.all_to_all(chosen, "expert", split_axis=0, concat_axis=0, tiled=True)
    return arrived.reshape(state.shape)


def perfect_matchings(members):
    if not members:
        return [()]
    first, rest = members[0], members[1:]
    found = []
    for at, other in enumerate(rest):
        for tail in perfect_matchings(rest[:at] + rest[at + 1 :]):
            found.append(((first, other),) + tail)
    return found


def exchange(states, pair_match):
    group_size = lax.axis_size("expert")
    matchings = perfect_matchings(tuple(range(group_size)))
    scale = [group_size**place for place in range(group_size)]
    keys = [sum(scale[a] * b + scale[b] * a for a, b in pairs) for pairs in matchings]
    key = jnp.sum(pair_match * jnp.array(scale, jnp.int32))
    branch = jnp.argmax(jnp.array(keys, jnp.int32) == key).astype(jnp.int32)

    def swap(pairs):
        perm = [(a, b) for a, b in pairs] + [(b, a) for a, b in pairs]
        return lambda values: tuple(lax.ppermute(value, "expert", perm) for value in values)

    return lax.switch(branch, [swap(pairs) for pairs in matchings], tuple(states))


def routed_gradient(tokens, cotangent, dest_ids, gate_probs, up_full):
    group_size = lax.axis_size("expert")
    tok_rows, top_count = dest_ids.shape
    width = tokens.shape[1]
    capacity = 3 * tok_rows * top_count // (2 * group_size)
    total = tok_rows * top_count
    flat_ids = dest_ids.reshape(-1)
    picked = (flat_ids[:, None] == jnp.arange(group_size, dtype=jnp.int32)[None, :]).astype(
        jnp.int32
    )
    ranking = jnp.sum((jnp.cumsum(picked, axis=0) - 1) * picked, axis=1)
    slot_index = flat_ids * capacity + ranking
    source = (
        jnp.full((group_size * capacity,), total, jnp.int32)
        .at[slot_index]
        .set(jnp.arange(total, dtype=jnp.int32))
    )
    filled = source < total
    safe_source = jnp.minimum(source, total - 1)
    row_index = safe_source // top_count
    weights_row = jnp.where(filled, gate_probs.reshape(-1)[safe_source], jnp.float32(0.0))
    sent_tokens = jnp.where(filled[:, None], tokens[row_index], jnp.zeros((), jnp.bfloat16))
    sent_scaled = (weights_row[:, None] * cotangent[row_index].astype(jnp.float32)).astype(
        jnp.bfloat16
    )
    sent_tokens = sent_tokens.reshape(group_size, capacity, width)
    sent_scaled = sent_scaled.reshape(group_size, capacity, width)
    got_tokens, got_scaled = (
        lax.all_to_all(sent_tokens, "expert", split_axis=0, concat_axis=0, tiled=True),
        lax.all_to_all(sent_scaled, "expert", split_axis=0, concat_axis=0, tiled=True),
    )
    rows_tokens = got_tokens.reshape(-1, width)
    rows_scaled = got_scaled.reshape(-1, width)
    hidden = jax.nn.silu(
        jnp.dot(rows_tokens, up_full, preferred_element_type=jnp.float32)
    ).astype(jnp.bfloat16)
    return lax.dot_general(
        hidden, rows_scaled, (((0,), (0,)), ((), ())), preferred_element_type=jnp.float32
    )


def gather_group(tokens, cotangent, expert_ids, gate_probs):
    rows = lax.all_gather(jnp.stack((tokens, cotangent)), "expert", axis=1, tiled=True)
    routing = jnp.concatenate((gate_probs, expert_ids.astype(jnp.float32)), axis=1)
    routing = lax.all_gather(routing, "expert", axis=0, tiled=True)
    return rows, routing


def dense_gradient(rows, routing, up_full, expert):
    top_count = routing.shape[1] // 2
    all_gates, all_ids = routing[:, :top_count], routing[:, top_count:]
    chosen = all_ids == expert.astype(jnp.float32)
    weights_row = jnp.sum(jnp.where(chosen, all_gates, jnp.float32(0.0)), axis=1)
    scaled = (weights_row[:, None] * rows[1].astype(jnp.float32)).astype(jnp.bfloat16)
    hidden = jax.nn.silu(
        jnp.dot(rows[0], up_full, preferred_element_type=jnp.float32)
    ).astype(jnp.bfloat16)
    return lax.dot_general(
        hidden, scaled, (((0,), (0,)), ((), ())), preferred_element_type=jnp.float32
    )


def grid_reduce_scatter(halves):
    where = lax.axis_index("dp")
    low, high = where % 2, where // 2
    size = lax.axis_size("dp")
    flip_low = [(d, d ^ 1) for d in range(size)]
    flip_high = [(d, d ^ 2) for d in range(size)]
    first, second = (half.reshape((2, 2, -1) + half.shape[1:]) for half in halves)
    sent = lax.ppermute(jnp.take(first, 1 - low, axis=1), "dp", flip_low)
    first = jnp.take(first, low, axis=1) + sent
    sent = lax.ppermute(jnp.take(second, 1 - high, axis=0), "dp", flip_high)
    second = jnp.take(second, high, axis=0) + sent
    sent = lax.ppermute(jnp.take(first, 1 - high, axis=0), "dp", flip_high)
    first = jnp.take(first, high, axis=0) + sent
    sent = lax.ppermute(jnp.take(second, 1 - low, axis=0), "dp", flip_low)
    second = jnp.take(second, low, axis=0) + sent
    return jnp.concatenate((first, second), axis=1)


def lamb_step(weight, moment_one, moment_two, gradient):
    first = beta_one * moment_one + (1.0 - beta_one) * gradient
    second = beta_two * moment_two + (1.0 - beta_two) * gradient * gradient
    update = first / (jnp.sqrt(second) + epsilon)
    weight_sq, update_sq = lax.psum((jnp.sum(weight * weight), jnp.sum(update * update)), "dp")
    trust_ratio = jnp.sqrt(weight_sq) / (jnp.sqrt(update_sq) + epsilon)
    renewed = weight - learn_rate * trust_ratio * update
    return (renewed, first, second)


def local(
    tokens, cotangent, expert_ids, gate_probs, up_weight, down_weight, moment1, moment2, pair_match
):
    group_size = lax.axis_size("expert")
    partner = pair_match[lax.axis_index("expert")]
    if group_size <= exchange_group_max and group_size * tokens.shape[0] <= dense_rows_max:
        rows, routing = gather_group(tokens, cotangent, expert_ids, gate_probs)
        up_local, weight = exchange((up_weight[0], down_weight[0]), pair_match)
        rows, up_local = lax.optimization_barrier((rows, up_local))
        up_full = lax.all_gather(up_local, "dp", axis=1, tiled=True)
        partial = dense_gradient(rows, routing, up_full, partner)
        moments, partial = lax.optimization_barrier(((moment1[0], moment2[0]), partial))
        (swapped,) = exchange((jnp.stack(moments),), pair_match)
        moment_one, moment_two = swapped[0], swapped[1]
        gradient = lax.psum_scatter(partial, "dp", scatter_dimension=0, tiled=True)
    else:
        up_local = relocate(up_weight[0], pair_match)
        up_full = lax.all_gather(up_local, "dp", axis=1, tiled=True)
        partial = routed_gradient(tokens, cotangent, pair_match[expert_ids], gate_probs, up_full)
        weight, moment_one, moment_two = (
            relocate(x[0], pair_match) for x in (down_weight, moment1, moment2)
        )
        if lax.axis_size("dp") == 4 and partial.shape[0] % 4 == 0:
            middle = partial.shape[1] // 2
            gradient = grid_reduce_scatter((partial[:, :middle], partial[:, middle:]))
        else:
            gradient = lax.psum_scatter(partial, "dp", scatter_dimension=0, tiled=True)
    renewed, first, second = lamb_step(weight, moment_one, moment_two, gradient)
    return (renewed[None], first[None], second[None])


def solution(mesh):
    in_specs = (
        P(("dp", "expert"), None),
        P(("dp", "expert"), None),
        P(("dp", "expert"), None),
        P(("dp", "expert"), None),
        P("expert", None, "dp"),
        P("expert", "dp", None),
        P("expert", "dp", None),
        P("expert", "dp", None),
        P(),
    )
    out_specs = (P("expert", "dp", None), P("expert", "dp", None), P("expert", "dp", None))
    return jax.shard_map(local, mesh=mesh, in_specs=in_specs, out_specs=out_specs, check_vma=False)
```

```python
import jax
import jax.numpy as jnp
from jax import lax
from jax.sharding import PartitionSpec as P

beta_one = 0.9
beta_two = 0.999
epsilon = 1e-06
learn_rate = 0.05

dense_rows_max = 2048
exchange_group_max = 8


def relocate(state, pair_match):
    group_size = lax.axis_size("expert")
    pieces = state.reshape((group_size, -1) + state.shape[1:])
    spread = lax.all_to_all(pieces, "expert", split_axis=0, concat_axis=0, tiled=True)
    chosen = jnp.take(spread, pair_match, axis=0)
    arrived = lax.all_to_all(chosen, "expert", split_axis=0, concat_axis=0, tiled=True)
    return arrived.reshape(state.shape)


def perfect_matchings(members):
    if not members:
        return [()]
    first, rest = members[0], members[1:]
    found = []
    for at, other in enumerate(rest):
        for tail in perfect_matchings(rest[:at] + rest[at + 1 :]):
            found.append(((first, other),) + tail)
    return found


def exchange(states, pair_match):
    group_size = lax.axis_size("expert")
    matchings = perfect_matchings(tuple(range(group_size)))
    scale = [group_size**place for place in range(group_size)]
    keys = [sum(scale[a] * b + scale[b] * a for a, b in pairs) for pairs in matchings]
    key = jnp.sum(pair_match * jnp.array(scale, jnp.int32))
    branch = jnp.argmax(jnp.array(keys, jnp.int32) == key).astype(jnp.int32)

    def swap(pairs):
        perm = [(a, b) for a, b in pairs] + [(b, a) for a, b in pairs]
        return lambda values: tuple(lax.ppermute(value, "expert", perm) for value in values)

    return lax.switch(branch, [swap(pairs) for pairs in matchings], tuple(states))


def routed_gradient(tokens, cotangent, dest_ids, gate_probs, up_full):
    group_size = lax.axis_size("expert")
    tok_rows, top_count = dest_ids.shape
    width = tokens.shape[1]
    capacity = 3 * tok_rows * top_count // (2 * group_size)
    total = tok_rows * top_count
    flat_ids = dest_ids.reshape(-1)
    picked = (flat_ids[:, None] == jnp.arange(group_size, dtype=jnp.int32)[None, :]).astype(
        jnp.int32
    )
    ranking = jnp.sum((jnp.cumsum(picked, axis=0) - 1) * picked, axis=1)
    slot_index = flat_ids * capacity + ranking
    source = (
        jnp.full((group_size * capacity,), total, jnp.int32)
        .at[slot_index]
        .set(jnp.arange(total, dtype=jnp.int32))
    )
    filled = source < total
    safe_source = jnp.minimum(source, total - 1)
    row_index = safe_source // top_count
    weights_row = jnp.where(filled, gate_probs.reshape(-1)[safe_source], jnp.float32(0.0))
    sent_tokens = jnp.where(filled[:, None], tokens[row_index], jnp.zeros((), jnp.bfloat16))
    sent_scaled = (weights_row[:, None] * cotangent[row_index].astype(jnp.float32)).astype(
        jnp.bfloat16
    )
    sent_tokens = sent_tokens.reshape(group_size, capacity, width)
    sent_scaled = sent_scaled.reshape(group_size, capacity, width)
    got_tokens, got_scaled = (
        lax.all_to_all(sent_tokens, "expert", split_axis=0, concat_axis=0, tiled=True),
        lax.all_to_all(sent_scaled, "expert", split_axis=0, concat_axis=0, tiled=True),
    )
    rows_tokens = got_tokens.reshape(-1, width)
    rows_scaled = got_scaled.reshape(-1, width)
    hidden = jax.nn.silu(
        jnp.dot(rows_tokens, up_full, preferred_element_type=jnp.float32)
    ).astype(jnp.bfloat16)
    return lax.dot_general(
        hidden, rows_scaled, (((0,), (0,)), ((), ())), preferred_element_type=jnp.float32
    )


def gather_group(tokens, cotangent, expert_ids, gate_probs):
    rows = lax.all_gather(jnp.stack((tokens, cotangent)), "expert", axis=1, tiled=True)
    routing = jnp.concatenate((gate_probs, expert_ids.astype(jnp.float32)), axis=1)
    routing = lax.all_gather(routing, "expert", axis=0, tiled=True)
    return rows, routing


def dense_gradient(rows, routing, up_full, expert):
    top_count = routing.shape[1] // 2
    all_gates, all_ids = routing[:, :top_count], routing[:, top_count:]
    chosen = all_ids == expert.astype(jnp.float32)
    weights_row = jnp.sum(jnp.where(chosen, all_gates, jnp.float32(0.0)), axis=1)
    scaled = (weights_row[:, None] * rows[1].astype(jnp.float32)).astype(jnp.bfloat16)
    hidden = jax.nn.silu(
        jnp.dot(rows[0], up_full, preferred_element_type=jnp.float32)
    ).astype(jnp.bfloat16)
    return lax.dot_general(
        hidden, scaled, (((0,), (0,)), ((), ())), preferred_element_type=jnp.float32
    )


def grid_reduce_scatter(halves):
    where = lax.axis_index("dp")
    low, high = where % 2, where // 2
    size = lax.axis_size("dp")
    flip_low = [(d, d ^ 1) for d in range(size)]
    flip_high = [(d, d ^ 2) for d in range(size)]
    first, second = (half.reshape((2, 2, -1) + half.shape[1:]) for half in halves)
    sent = lax.ppermute(jnp.take(first, 1 - low, axis=1), "dp", flip_low)
    first = jnp.take(first, low, axis=1) + sent
    sent = lax.ppermute(jnp.take(second, 1 - high, axis=0), "dp", flip_high)
    second = jnp.take(second, high, axis=0) + sent
    sent = lax.ppermute(jnp.take(first, 1 - high, axis=0), "dp", flip_high)
    first = jnp.take(first, high, axis=0) + sent
    sent = lax.ppermute(jnp.take(second, 1 - low, axis=0), "dp", flip_low)
    second = jnp.take(second, low, axis=0) + sent
    return jnp.concatenate((first, second), axis=1)


def lamb_step(weight, moment_one, moment_two, gradient):
    first = beta_one * moment_one + (1.0 - beta_one) * gradient
    second = beta_two * moment_two + (1.0 - beta_two) * gradient * gradient
    update = first / (jnp.sqrt(second) + epsilon)
    weight_sq, update_sq = lax.psum((jnp.sum(weight * weight), jnp.sum(update * update)), "dp")
    trust_ratio = jnp.sqrt(weight_sq) / (jnp.sqrt(update_sq) + epsilon)
    renewed = weight - learn_rate * trust_ratio * update
    return (renewed, first, second)


def local(
    tokens, cotangent, expert_ids, gate_probs, up_weight, down_weight, moment1, moment2, pair_match
):
    group_size = lax.axis_size("expert")
    partner = pair_match[lax.axis_index("expert")]
    if group_size <= exchange_group_max and group_size * tokens.shape[0] <= dense_rows_max:
        rows, routing = gather_group(tokens, cotangent, expert_ids, gate_probs)
        (up_local,) = exchange((up_weight[0],), pair_match)
        up_local, held_weight = lax.optimization_barrier((up_local, down_weight[0]))
        (weight,) = exchange((held_weight,), pair_match)
        rows, up_ready = lax.optimization_barrier((rows, up_local))
        up_full = lax.all_gather(up_ready, "dp", axis=1, tiled=True)
        up_full, weight = lax.optimization_barrier((up_full, weight))
        partial = dense_gradient(rows, routing, up_full, partner)
        moments, partial = lax.optimization_barrier(((moment1[0], moment2[0]), partial))
        (swapped,) = exchange((jnp.stack(moments),), pair_match)
        moment_one, moment_two = swapped[0], swapped[1]
        gradient = lax.psum_scatter(partial, "dp", scatter_dimension=0, tiled=True)
    else:
        up_local = relocate(up_weight[0], pair_match)
        up_full = lax.all_gather(up_local, "dp", axis=1, tiled=True)
        partial = routed_gradient(tokens, cotangent, pair_match[expert_ids], gate_probs, up_full)
        weight, moment_one, moment_two = (
            relocate(x[0], pair_match) for x in (down_weight, moment1, moment2)
        )
        if lax.axis_size("dp") == 4 and partial.shape[0] % 4 == 0:
            middle = partial.shape[1] // 2
            gradient = grid_reduce_scatter((partial[:, :middle], partial[:, middle:]))
        else:
            gradient = lax.psum_scatter(partial, "dp", scatter_dimension=0, tiled=True)
    renewed, first, second = lamb_step(weight, moment_one, moment_two, gradient)
    return (renewed[None], first[None], second[None])


def solution(mesh):
    in_specs = (
        P(("dp", "expert"), None),
        P(("dp", "expert"), None),
        P(("dp", "expert"), None),
        P(("dp", "expert"), None),
        P("expert", None, "dp"),
        P("expert", "dp", None),
        P("expert", "dp", None),
        P("expert", "dp", None),
        P(),
    )
    out_specs = (P("expert", "dp", None), P("expert", "dp", None), P("expert", "dp", None))
    return jax.shard_map(local, mesh=mesh, in_specs=in_specs, out_specs=out_specs, check_vma=False)
```

```python
import jax
import jax.numpy as jnp
from jax import lax
from jax.sharding import PartitionSpec as P

beta_one = 0.9
beta_two = 0.999
epsilon = 1e-06
learn_rate = 0.05

dense_rows_max = 2048
exchange_group_max = 8


def relocate(state, pair_match):
    group_size = lax.axis_size("expert")
    pieces = state.reshape((group_size, -1) + state.shape[1:])
    spread = lax.all_to_all(pieces, "expert", split_axis=0, concat_axis=0, tiled=True)
    chosen = jnp.take(spread, pair_match, axis=0)
    arrived = lax.all_to_all(chosen, "expert", split_axis=0, concat_axis=0, tiled=True)
    return arrived.reshape(state.shape)


def perfect_matchings(members):
    if not members:
        return [()]
    first, rest = members[0], members[1:]
    found = []
    for at, other in enumerate(rest):
        for tail in perfect_matchings(rest[:at] + rest[at + 1 :]):
            found.append(((first, other),) + tail)
    return found


def exchange(states, pair_match):
    group_size = lax.axis_size("expert")
    matchings = perfect_matchings(tuple(range(group_size)))
    scale = [group_size**place for place in range(group_size)]
    keys = [sum(scale[a] * b + scale[b] * a for a, b in pairs) for pairs in matchings]
    key = jnp.sum(pair_match * jnp.array(scale, jnp.int32))
    branch = jnp.argmax(jnp.array(keys, jnp.int32) == key).astype(jnp.int32)

    def swap(pairs):
        perm = [(a, b) for a, b in pairs] + [(b, a) for a, b in pairs]
        return lambda values: tuple(lax.ppermute(value, "expert", perm) for value in values)

    return lax.switch(branch, [swap(pairs) for pairs in matchings], tuple(states))


def routed_gradient(tokens, cotangent, dest_ids, gate_probs, up_full):
    group_size = lax.axis_size("expert")
    tok_rows, top_count = dest_ids.shape
    width = tokens.shape[1]
    capacity = 3 * tok_rows * top_count // (2 * group_size)
    total = tok_rows * top_count
    flat_ids = dest_ids.reshape(-1)
    picked = (flat_ids[:, None] == jnp.arange(group_size, dtype=jnp.int32)[None, :]).astype(
        jnp.int32
    )
    ranking = jnp.sum((jnp.cumsum(picked, axis=0) - 1) * picked, axis=1)
    slot_index = flat_ids * capacity + ranking
    source = (
        jnp.full((group_size * capacity,), total, jnp.int32)
        .at[slot_index]
        .set(jnp.arange(total, dtype=jnp.int32))
    )
    filled = source < total
    safe_source = jnp.minimum(source, total - 1)
    row_index = safe_source // top_count
    weights_row = jnp.where(filled, gate_probs.reshape(-1)[safe_source], jnp.float32(0.0))
    sent_tokens = jnp.where(filled[:, None], tokens[row_index], jnp.zeros((), jnp.bfloat16))
    sent_scaled = (weights_row[:, None] * cotangent[row_index].astype(jnp.float32)).astype(
        jnp.bfloat16
    )
    sent_tokens = sent_tokens.reshape(group_size, capacity, width)
    sent_scaled = sent_scaled.reshape(group_size, capacity, width)
    got_tokens, got_scaled = (
        lax.all_to_all(sent_tokens, "expert", split_axis=0, concat_axis=0, tiled=True),
        lax.all_to_all(sent_scaled, "expert", split_axis=0, concat_axis=0, tiled=True),
    )
    rows_tokens = got_tokens.reshape(-1, width)
    rows_scaled = got_scaled.reshape(-1, width)
    hidden = jax.nn.silu(
        jnp.dot(rows_tokens, up_full, preferred_element_type=jnp.float32)
    ).astype(jnp.bfloat16)
    return lax.dot_general(
        hidden, rows_scaled, (((0,), (0,)), ((), ())), preferred_element_type=jnp.float32
    )


def gather_group(tokens, cotangent, expert_ids, gate_probs):
    rows = lax.all_gather(jnp.stack((tokens, cotangent)), "expert", axis=1, tiled=True)
    routing = jnp.concatenate((gate_probs, expert_ids.astype(jnp.float32)), axis=1)
    routing = lax.all_gather(routing, "expert", axis=0, tiled=True)
    return rows, routing


def dense_gradient(rows, routing, up_full, expert):
    top_count = routing.shape[1] // 2
    all_gates, all_ids = routing[:, :top_count], routing[:, top_count:]
    chosen = all_ids == expert.astype(jnp.float32)
    weights_row = jnp.sum(jnp.where(chosen, all_gates, jnp.float32(0.0)), axis=1)
    scaled = (weights_row[:, None] * rows[1].astype(jnp.float32)).astype(jnp.bfloat16)
    hidden = jax.nn.silu(
        jnp.dot(rows[0], up_full, preferred_element_type=jnp.float32)
    ).astype(jnp.bfloat16)
    return lax.dot_general(
        hidden, scaled, (((0,), (0,)), ((), ())), preferred_element_type=jnp.float32
    )


def grid_reduce_scatter(halves):
    where = lax.axis_index("dp")
    low, high = where % 2, where // 2
    size = lax.axis_size("dp")
    flip_low = [(d, d ^ 1) for d in range(size)]
    flip_high = [(d, d ^ 2) for d in range(size)]
    first, second = (half.reshape((2, 2, -1) + half.shape[1:]) for half in halves)
    sent = lax.ppermute(jnp.take(first, 1 - low, axis=1), "dp", flip_low)
    first = jnp.take(first, low, axis=1) + sent
    sent = lax.ppermute(jnp.take(second, 1 - high, axis=0), "dp", flip_high)
    second = jnp.take(second, high, axis=0) + sent
    sent = lax.ppermute(jnp.take(first, 1 - high, axis=0), "dp", flip_high)
    first = jnp.take(first, high, axis=0) + sent
    sent = lax.ppermute(jnp.take(second, 1 - low, axis=0), "dp", flip_low)
    second = jnp.take(second, low, axis=0) + sent
    return jnp.concatenate((first, second), axis=1)


def lamb_step(weight, moment_one, moment_two, gradient):
    first = beta_one * moment_one + (1.0 - beta_one) * gradient
    second = beta_two * moment_two + (1.0 - beta_two) * gradient * gradient
    update = first / (jnp.sqrt(second) + epsilon)
    weight_sq, update_sq = lax.psum((jnp.sum(weight * weight), jnp.sum(update * update)), "dp")
    trust_ratio = jnp.sqrt(weight_sq) / (jnp.sqrt(update_sq) + epsilon)
    renewed = weight - learn_rate * trust_ratio * update
    return (renewed, first, second)


def local(
    tokens, cotangent, expert_ids, gate_probs, up_weight, down_weight, moment1, moment2, pair_match
):
    group_size = lax.axis_size("expert")
    partner = pair_match[lax.axis_index("expert")]
    if group_size <= exchange_group_max and group_size * tokens.shape[0] <= dense_rows_max:
        rows, routing = gather_group(tokens, cotangent, expert_ids, gate_probs)
        routing, up_held = lax.optimization_barrier((routing, up_weight[0]))
        (up_local,) = exchange((up_held,), pair_match)
        up_local, held_weight = lax.optimization_barrier((up_local, down_weight[0]))
        (weight,) = exchange((held_weight,), pair_match)
        rows, up_ready = lax.optimization_barrier((rows, up_local))
        up_full = lax.all_gather(up_ready, "dp", axis=1, tiled=True)
        up_full, weight = lax.optimization_barrier((up_full, weight))
        partial = dense_gradient(rows, routing, up_full, partner)
        moments, partial = lax.optimization_barrier(((moment1[0], moment2[0]), partial))
        (swapped,) = exchange((jnp.stack(moments),), pair_match)
        moment_one, moment_two = swapped[0], swapped[1]
        gradient = lax.psum_scatter(partial, "dp", scatter_dimension=0, tiled=True)
    else:
        up_local = relocate(up_weight[0], pair_match)
        up_full = lax.all_gather(up_local, "dp", axis=1, tiled=True)
        partial = routed_gradient(tokens, cotangent, pair_match[expert_ids], gate_probs, up_full)
        weight, moment_one, moment_two = (
            relocate(x[0], pair_match) for x in (down_weight, moment1, moment2)
        )
        if lax.axis_size("dp") == 4 and partial.shape[0] % 4 == 0:
            middle = partial.shape[1] // 2
            gradient = grid_reduce_scatter((partial[:, :middle], partial[:, middle:]))
        else:
            gradient = lax.psum_scatter(partial, "dp", scatter_dimension=0, tiled=True)
    renewed, first, second = lamb_step(weight, moment_one, moment_two, gradient)
    return (renewed[None], first[None], second[None])


def solution(mesh):
    in_specs = (
        P(("dp", "expert"), None),
        P(("dp", "expert"), None),
        P(("dp", "expert"), None),
        P(("dp", "expert"), None),
        P("expert", None, "dp"),
        P("expert", "dp", None),
        P("expert", "dp", None),
        P("expert", "dp", None),
        P(),
    )
    out_specs = (P("expert", "dp", None), P("expert", "dp", None), P("expert", "dp", None))
    return jax.shard_map(local, mesh=mesh, in_specs=in_specs, out_specs=out_specs, check_vma=False)
```

```python
import jax
import jax.numpy as jnp
from jax import lax
from jax.sharding import PartitionSpec as P

beta_one = 0.9
beta_two = 0.999
epsilon = 1e-06
learn_rate = 0.05

dense_rows_max = 2048
exchange_group_max = 8


def relocate(state, pair_match):
    group_size = lax.axis_size("expert")
    pieces = state.reshape((group_size, -1) + state.shape[1:])
    spread = lax.all_to_all(pieces, "expert", split_axis=0, concat_axis=0, tiled=True)
    chosen = jnp.take(spread, pair_match, axis=0)
    arrived = lax.all_to_all(chosen, "expert", split_axis=0, concat_axis=0, tiled=True)
    return arrived.reshape(state.shape)


def perfect_matchings(members):
    if not members:
        return [()]
    first, rest = members[0], members[1:]
    found = []
    for at, other in enumerate(rest):
        for tail in perfect_matchings(rest[:at] + rest[at + 1 :]):
            found.append(((first, other),) + tail)
    return found


def exchange(states, pair_match):
    group_size = lax.axis_size("expert")
    matchings = perfect_matchings(tuple(range(group_size)))
    scale = [group_size**place for place in range(group_size)]
    keys = [sum(scale[a] * b + scale[b] * a for a, b in pairs) for pairs in matchings]
    key = jnp.sum(pair_match * jnp.array(scale, jnp.int32))
    branch = jnp.argmax(jnp.array(keys, jnp.int32) == key).astype(jnp.int32)

    def swap(pairs):
        perm = [(a, b) for a, b in pairs] + [(b, a) for a, b in pairs]
        return lambda values: tuple(lax.ppermute(value, "expert", perm) for value in values)

    return lax.switch(branch, [swap(pairs) for pairs in matchings], tuple(states))


def routed_gradient(tokens, cotangent, dest_ids, gate_probs, up_full):
    group_size = lax.axis_size("expert")
    tok_rows, top_count = dest_ids.shape
    width = tokens.shape[1]
    capacity = 3 * tok_rows * top_count // (2 * group_size)
    total = tok_rows * top_count
    flat_ids = dest_ids.reshape(-1)
    picked = (flat_ids[:, None] == jnp.arange(group_size, dtype=jnp.int32)[None, :]).astype(
        jnp.int32
    )
    ranking = jnp.sum((jnp.cumsum(picked, axis=0) - 1) * picked, axis=1)
    slot_index = flat_ids * capacity + ranking
    source = (
        jnp.full((group_size * capacity,), total, jnp.int32)
        .at[slot_index]
        .set(jnp.arange(total, dtype=jnp.int32))
    )
    filled = source < total
    safe_source = jnp.minimum(source, total - 1)
    row_index = safe_source // top_count
    weights_row = jnp.where(filled, gate_probs.reshape(-1)[safe_source], jnp.float32(0.0))
    sent_tokens = jnp.where(filled[:, None], tokens[row_index], jnp.zeros((), jnp.bfloat16))
    sent_scaled = (weights_row[:, None] * cotangent[row_index].astype(jnp.float32)).astype(
        jnp.bfloat16
    )
    sent_tokens = sent_tokens.reshape(group_size, capacity, width)
    sent_scaled = sent_scaled.reshape(group_size, capacity, width)
    got_tokens, got_scaled = (
        lax.all_to_all(sent_tokens, "expert", split_axis=0, concat_axis=0, tiled=True),
        lax.all_to_all(sent_scaled, "expert", split_axis=0, concat_axis=0, tiled=True),
    )
    rows_tokens = got_tokens.reshape(-1, width)
    rows_scaled = got_scaled.reshape(-1, width)
    hidden = jax.nn.silu(
        jnp.dot(rows_tokens, up_full, preferred_element_type=jnp.float32)
    ).astype(jnp.bfloat16)
    return lax.dot_general(
        hidden, rows_scaled, (((0,), (0,)), ((), ())), preferred_element_type=jnp.float32
    )


def gather_group(tokens, cotangent, expert_ids, gate_probs):
    rows = lax.all_gather(jnp.stack((tokens, cotangent)), "expert", axis=1, tiled=True)
    routing = jnp.concatenate((gate_probs, expert_ids.astype(jnp.float32)), axis=1)
    routing = lax.all_gather(routing, "expert", axis=0, tiled=True)
    return rows, routing


def dense_gradient(rows, routing, up_full, expert):
    top_count = routing.shape[1] // 2
    all_gates, all_ids = routing[:, :top_count], routing[:, top_count:]
    chosen = all_ids == expert.astype(jnp.float32)
    weights_row = jnp.sum(jnp.where(chosen, all_gates, jnp.float32(0.0)), axis=1)
    scaled = (weights_row[:, None] * rows[1].astype(jnp.float32)).astype(jnp.bfloat16)
    hidden = jax.nn.silu(
        jnp.dot(rows[0], up_full, preferred_element_type=jnp.float32)
    ).astype(jnp.bfloat16)
    return lax.dot_general(
        hidden, scaled, (((0,), (0,)), ((), ())), preferred_element_type=jnp.float32
    )


def grid_all_gather(part):
    where = lax.axis_index("dp")
    low, high = where % 2, where // 2
    size = lax.axis_size("dp")
    other = lax.ppermute(part, "dp", [(d, d ^ 1) for d in range(size)])
    pair = jnp.where(low == 0, jnp.concatenate((part, other), axis=1),
                     jnp.concatenate((other, part), axis=1))
    other = lax.ppermute(pair, "dp", [(d, d ^ 2) for d in range(size)])
    return jnp.where(high == 0, jnp.concatenate((pair, other), axis=1),
                     jnp.concatenate((other, pair), axis=1))


def grid_reduce_scatter(halves):
    where = lax.axis_index("dp")
    low, high = where % 2, where // 2
    size = lax.axis_size("dp")
    flip_low = [(d, d ^ 1) for d in range(size)]
    flip_high = [(d, d ^ 2) for d in range(size)]
    first, second = (half.reshape((2, 2, -1) + half.shape[1:]) for half in halves)
    sent = lax.ppermute(jnp.take(first, 1 - low, axis=1), "dp", flip_low)
    first = jnp.take(first, low, axis=1) + sent
    sent = lax.ppermute(jnp.take(second, 1 - high, axis=0), "dp", flip_high)
    second = jnp.take(second, high, axis=0) + sent
    sent = lax.ppermute(jnp.take(first, 1 - high, axis=0), "dp", flip_high)
    first = jnp.take(first, high, axis=0) + sent
    sent = lax.ppermute(jnp.take(second, 1 - low, axis=0), "dp", flip_low)
    second = jnp.take(second, low, axis=0) + sent
    return jnp.concatenate((first, second), axis=1)


def lamb_step(weight, moment_one, moment_two, gradient):
    first = beta_one * moment_one + (1.0 - beta_one) * gradient
    second = beta_two * moment_two + (1.0 - beta_two) * gradient * gradient
    update = first / (jnp.sqrt(second) + epsilon)
    weight_sq, update_sq = lax.psum((jnp.sum(weight * weight), jnp.sum(update * update)), "dp")
    trust_ratio = jnp.sqrt(weight_sq) / (jnp.sqrt(update_sq) + epsilon)
    renewed = weight - learn_rate * trust_ratio * update
    return (renewed, first, second)


def local(
    tokens, cotangent, expert_ids, gate_probs, up_weight, down_weight, moment1, moment2, pair_match
):
    group_size = lax.axis_size("expert")
    partner = pair_match[lax.axis_index("expert")]
    if group_size <= exchange_group_max and group_size * tokens.shape[0] <= dense_rows_max:
        rows, routing = gather_group(tokens, cotangent, expert_ids, gate_probs)
        routing, up_held = lax.optimization_barrier((routing, up_weight[0]))
        (up_local,) = exchange((up_held,), pair_match)
        up_local, held_weight = lax.optimization_barrier((up_local, down_weight[0]))
        (weight,) = exchange((held_weight,), pair_match)
        if lax.axis_size("dp") == 4:
            up_full = grid_all_gather(up_local)
        else:
            up_full = lax.all_gather(up_local, "dp", axis=1, tiled=True)
        up_full, weight = lax.optimization_barrier((up_full, weight))
        partial = dense_gradient(rows, routing, up_full, partner)
        moments, partial = lax.optimization_barrier(((moment1[0], moment2[0]), partial))
        (swapped,) = exchange((jnp.stack(moments),), pair_match)
        moment_one, moment_two = swapped[0], swapped[1]
        gradient = lax.psum_scatter(partial, "dp", scatter_dimension=0, tiled=True)
    else:
        up_local = relocate(up_weight[0], pair_match)
        up_full = lax.all_gather(up_local, "dp", axis=1, tiled=True)
        partial = routed_gradient(tokens, cotangent, pair_match[expert_ids], gate_probs, up_full)
        weight, moment_one, moment_two = (
            relocate(x[0], pair_match) for x in (down_weight, moment1, moment2)
        )
        if lax.axis_size("dp") == 4 and partial.shape[0] % 4 == 0:
            middle = partial.shape[1] // 2
            gradient = grid_reduce_scatter((partial[:, :middle], partial[:, middle:]))
        else:
            gradient = lax.psum_scatter(partial, "dp", scatter_dimension=0, tiled=True)
    renewed, first, second = lamb_step(weight, moment_one, moment_two, gradient)
    return (renewed[None], first[None], second[None])


def solution(mesh):
    in_specs = (
        P(("dp", "expert"), None),
        P(("dp", "expert"), None),
        P(("dp", "expert"), None),
        P(("dp", "expert"), None),
        P("expert", None, "dp"),
        P("expert", "dp", None),
        P("expert", "dp", None),
        P("expert", "dp", None),
        P(),
    )
    out_specs = (P("expert", "dp", None), P("expert", "dp", None), P("expert", "dp", None))
    return jax.shard_map(local, mesh=mesh, in_specs=in_specs, out_specs=out_specs, check_vma=False)
```

```python
import jax
import jax.numpy as jnp
from jax import lax
from jax.sharding import PartitionSpec as P

beta_one = 0.9
beta_two = 0.999
epsilon = 1e-06
learn_rate = 0.05

dense_rows_max = 2048
exchange_group_max = 8


def relocate(state, pair_match):
    group_size = lax.axis_size("expert")
    pieces = state.reshape((group_size, -1) + state.shape[1:])
    spread = lax.all_to_all(pieces, "expert", split_axis=0, concat_axis=0, tiled=True)
    chosen = jnp.take(spread, pair_match, axis=0)
    arrived = lax.all_to_all(chosen, "expert", split_axis=0, concat_axis=0, tiled=True)
    return arrived.reshape(state.shape)


def perfect_matchings(members):
    if not members:
        return [()]
    first, rest = members[0], members[1:]
    found = []
    for at, other in enumerate(rest):
        for tail in perfect_matchings(rest[:at] + rest[at + 1 :]):
            found.append(((first, other),) + tail)
    return found


def exchange(states, pair_match):
    group_size = lax.axis_size("expert")
    matchings = perfect_matchings(tuple(range(group_size)))
    scale = [group_size**place for place in range(group_size)]
    keys = [sum(scale[a] * b + scale[b] * a for a, b in pairs) for pairs in matchings]
    key = jnp.sum(pair_match * jnp.array(scale, jnp.int32))
    branch = jnp.argmax(jnp.array(keys, jnp.int32) == key).astype(jnp.int32)

    def swap(pairs):
        perm = [(a, b) for a, b in pairs] + [(b, a) for a, b in pairs]
        return lambda values: tuple(lax.ppermute(value, "expert", perm) for value in values)

    return lax.switch(branch, [swap(pairs) for pairs in matchings], tuple(states))


def routed_gradient(tokens, cotangent, dest_ids, gate_probs, up_full):
    group_size = lax.axis_size("expert")
    tok_rows, top_count = dest_ids.shape
    width = tokens.shape[1]
    capacity = 3 * tok_rows * top_count // (2 * group_size)
    total = tok_rows * top_count
    flat_ids = dest_ids.reshape(-1)
    picked = (flat_ids[:, None] == jnp.arange(group_size, dtype=jnp.int32)[None, :]).astype(
        jnp.int32
    )
    ranking = jnp.sum((jnp.cumsum(picked, axis=0) - 1) * picked, axis=1)
    slot_index = flat_ids * capacity + ranking
    source = (
        jnp.full((group_size * capacity,), total, jnp.int32)
        .at[slot_index]
        .set(jnp.arange(total, dtype=jnp.int32))
    )
    filled = source < total
    safe_source = jnp.minimum(source, total - 1)
    row_index = safe_source // top_count
    weights_row = jnp.where(filled, gate_probs.reshape(-1)[safe_source], jnp.float32(0.0))
    sent_tokens = jnp.where(filled[:, None], tokens[row_index], jnp.zeros((), jnp.bfloat16))
    sent_scaled = (weights_row[:, None] * cotangent[row_index].astype(jnp.float32)).astype(
        jnp.bfloat16
    )
    sent_tokens = sent_tokens.reshape(group_size, capacity, width)
    sent_scaled = sent_scaled.reshape(group_size, capacity, width)
    got_tokens, got_scaled = (
        lax.all_to_all(sent_tokens, "expert", split_axis=0, concat_axis=0, tiled=True),
        lax.all_to_all(sent_scaled, "expert", split_axis=0, concat_axis=0, tiled=True),
    )
    rows_tokens = got_tokens.reshape(-1, width)
    rows_scaled = got_scaled.reshape(-1, width)
    hidden = jax.nn.silu(
        jnp.dot(rows_tokens, up_full, preferred_element_type=jnp.float32)
    ).astype(jnp.bfloat16)
    return lax.dot_general(
        hidden, rows_scaled, (((0,), (0,)), ((), ())), preferred_element_type=jnp.float32
    )


def gather_group(tokens, cotangent, expert_ids, gate_probs):
    rows = lax.all_gather(jnp.stack((tokens, cotangent)), "expert", axis=1, tiled=True)
    routing = jnp.concatenate((gate_probs, expert_ids.astype(jnp.float32)), axis=1)
    routing = lax.all_gather(routing, "expert", axis=0, tiled=True)
    return rows, routing


def dense_gradient(rows, routing, up_full, expert):
    top_count = routing.shape[1] // 2
    all_gates, all_ids = routing[:, :top_count], routing[:, top_count:]
    chosen = all_ids == expert.astype(jnp.float32)
    weights_row = jnp.sum(jnp.where(chosen, all_gates, jnp.float32(0.0)), axis=1)
    scaled = (weights_row[:, None] * rows[1].astype(jnp.float32)).astype(jnp.bfloat16)
    hidden = jax.nn.silu(
        jnp.dot(rows[0], up_full, preferred_element_type=jnp.float32)
    ).astype(jnp.bfloat16)
    return lax.dot_general(
        hidden, scaled, (((0,), (0,)), ((), ())), preferred_element_type=jnp.float32
    )


def grid_reduce_scatter(halves):
    where = lax.axis_index("dp")
    low, high = where % 2, where // 2
    size = lax.axis_size("dp")
    flip_low = [(d, d ^ 1) for d in range(size)]
    flip_high = [(d, d ^ 2) for d in range(size)]
    first, second = (half.reshape((2, 2, -1) + half.shape[1:]) for half in halves)
    sent = lax.ppermute(jnp.take(first, 1 - low, axis=1), "dp", flip_low)
    first = jnp.take(first, low, axis=1) + sent
    sent = lax.ppermute(jnp.take(second, 1 - high, axis=0), "dp", flip_high)
    second = jnp.take(second, high, axis=0) + sent
    sent = lax.ppermute(jnp.take(first, 1 - high, axis=0), "dp", flip_high)
    first = jnp.take(first, high, axis=0) + sent
    sent = lax.ppermute(jnp.take(second, 1 - low, axis=0), "dp", flip_low)
    second = jnp.take(second, low, axis=0) + sent
    return jnp.concatenate((first, second), axis=1)


def lamb_step(weight, moment_one, moment_two, gradient):
    first = beta_one * moment_one + (1.0 - beta_one) * gradient
    second = beta_two * moment_two + (1.0 - beta_two) * gradient * gradient
    update = first / (jnp.sqrt(second) + epsilon)
    sums = jnp.stack((jnp.sum(weight * weight), jnp.sum(update * update)))
    size = lax.axis_size("dp")
    if size == 4:
        for flip in (1, 2):
            sums = sums + lax.ppermute(sums, "dp", [(d, d ^ flip) for d in range(size)])
    else:
        sums = lax.psum(sums, "dp")
    weight_sq, update_sq = sums[0], sums[1]
    trust_ratio = jnp.sqrt(weight_sq) / (jnp.sqrt(update_sq) + epsilon)
    renewed = weight - learn_rate * trust_ratio * update
    return (renewed, first, second)


def local(
    tokens, cotangent, expert_ids, gate_probs, up_weight, down_weight, moment1, moment2, pair_match
):
    group_size = lax.axis_size("expert")
    partner = pair_match[lax.axis_index("expert")]
    if group_size <= exchange_group_max and group_size * tokens.shape[0] <= dense_rows_max:
        rows, routing = gather_group(tokens, cotangent, expert_ids, gate_probs)
        routing, up_held = lax.optimization_barrier((routing, up_weight[0]))
        (up_local,) = exchange((up_held,), pair_match)
        up_local, held_weight = lax.optimization_barrier((up_local, down_weight[0]))
        (weight,) = exchange((held_weight,), pair_match)
        rows, up_ready = lax.optimization_barrier((rows, up_local))
        up_full = lax.all_gather(up_ready, "dp", axis=1, tiled=True)
        up_full, weight = lax.optimization_barrier((up_full, weight))
        partial = dense_gradient(rows, routing, up_full, partner)
        moments, partial = lax.optimization_barrier(((moment1[0], moment2[0]), partial))
        (swapped,) = exchange((jnp.stack(moments),), pair_match)
        moment_one, moment_two = swapped[0], swapped[1]
        gradient = lax.psum_scatter(partial, "dp", scatter_dimension=0, tiled=True)
    else:
        up_local = relocate(up_weight[0], pair_match)
        up_full = lax.all_gather(up_local, "dp", axis=1, tiled=True)
        partial = routed_gradient(tokens, cotangent, pair_match[expert_ids], gate_probs, up_full)
        weight, moment_one, moment_two = (
            relocate(x[0], pair_match) for x in (down_weight, moment1, moment2)
        )
        if lax.axis_size("dp") == 4 and partial.shape[0] % 4 == 0:
            middle = partial.shape[1] // 2
            gradient = grid_reduce_scatter((partial[:, :middle], partial[:, middle:]))
        else:
            gradient = lax.psum_scatter(partial, "dp", scatter_dimension=0, tiled=True)
    renewed, first, second = lamb_step(weight, moment_one, moment_two, gradient)
    return (renewed[None], first[None], second[None])


def solution(mesh):
    in_specs = (
        P(("dp", "expert"), None),
        P(("dp", "expert"), None),
        P(("dp", "expert"), None),
        P(("dp", "expert"), None),
        P("expert", None, "dp"),
        P("expert", "dp", None),
        P("expert", "dp", None),
        P("expert", "dp", None),
        P(),
    )
    out_specs = (P("expert", "dp", None), P("expert", "dp", None), P("expert", "dp", None))
    return jax.shard_map(local, mesh=mesh, in_specs=in_specs, out_specs=out_specs, check_vma=False)
```

```python
import jax
import jax.numpy as jnp
from jax import lax
from jax.sharding import PartitionSpec as P

beta_one = 0.9
beta_two = 0.999
epsilon = 1e-06
learn_rate = 0.05

dense_rows_max = 2048
exchange_group_max = 8


def relocate(state, pair_match):
    group_size = lax.axis_size("expert")
    pieces = state.reshape((group_size, -1) + state.shape[1:])
    spread = lax.all_to_all(pieces, "expert", split_axis=0, concat_axis=0, tiled=True)
    chosen = jnp.take(spread, pair_match, axis=0)
    arrived = lax.all_to_all(chosen, "expert", split_axis=0, concat_axis=0, tiled=True)
    return arrived.reshape(state.shape)


def perfect_matchings(members):
    if not members:
        return [()]
    first, rest = members[0], members[1:]
    found = []
    for at, other in enumerate(rest):
        for tail in perfect_matchings(rest[:at] + rest[at + 1 :]):
            found.append(((first, other),) + tail)
    return found


def exchange(states, pair_match):
    group_size = lax.axis_size("expert")
    matchings = perfect_matchings(tuple(range(group_size)))
    scale = [group_size**place for place in range(group_size)]
    keys = [sum(scale[a] * b + scale[b] * a for a, b in pairs) for pairs in matchings]
    key = jnp.sum(pair_match * jnp.array(scale, jnp.int32))
    branch = jnp.argmax(jnp.array(keys, jnp.int32) == key).astype(jnp.int32)

    def swap(pairs):
        perm = [(a, b) for a, b in pairs] + [(b, a) for a, b in pairs]
        return lambda values: tuple(lax.ppermute(value, "expert", perm) for value in values)

    return lax.switch(branch, [swap(pairs) for pairs in matchings], tuple(states))


def routed_gradient(tokens, cotangent, dest_ids, gate_probs, up_full):
    group_size = lax.axis_size("expert")
    tok_rows, top_count = dest_ids.shape
    width = tokens.shape[1]
    capacity = 3 * tok_rows * top_count // (2 * group_size)
    total = tok_rows * top_count
    flat_ids = dest_ids.reshape(-1)
    picked = (flat_ids[:, None] == jnp.arange(group_size, dtype=jnp.int32)[None, :]).astype(
        jnp.int32
    )
    ranking = jnp.sum((jnp.cumsum(picked, axis=0) - 1) * picked, axis=1)
    slot_index = flat_ids * capacity + ranking
    source = (
        jnp.full((group_size * capacity,), total, jnp.int32)
        .at[slot_index]
        .set(jnp.arange(total, dtype=jnp.int32))
    )
    filled = source < total
    safe_source = jnp.minimum(source, total - 1)
    row_index = safe_source // top_count
    weights_row = jnp.where(filled, gate_probs.reshape(-1)[safe_source], jnp.float32(0.0))
    sent_tokens = jnp.where(filled[:, None], tokens[row_index], jnp.zeros((), jnp.bfloat16))
    sent_scaled = (weights_row[:, None] * cotangent[row_index].astype(jnp.float32)).astype(
        jnp.bfloat16
    )
    sent_tokens = sent_tokens.reshape(group_size, capacity, width)
    sent_scaled = sent_scaled.reshape(group_size, capacity, width)
    got_tokens, got_scaled = (
        lax.all_to_all(sent_tokens, "expert", split_axis=0, concat_axis=0, tiled=True),
        lax.all_to_all(sent_scaled, "expert", split_axis=0, concat_axis=0, tiled=True),
    )
    rows_tokens = got_tokens.reshape(-1, width)
    rows_scaled = got_scaled.reshape(-1, width)
    hidden = jax.nn.silu(
        jnp.dot(rows_tokens, up_full, preferred_element_type=jnp.float32)
    ).astype(jnp.bfloat16)
    return lax.dot_general(
        hidden, rows_scaled, (((0,), (0,)), ((), ())), preferred_element_type=jnp.float32
    )


def gather_group(tokens, cotangent, expert_ids, gate_probs):
    rows = lax.all_gather(jnp.stack((tokens, cotangent)), "expert", axis=1, tiled=True)
    routing = jnp.concatenate((gate_probs, expert_ids.astype(jnp.float32)), axis=1)
    routing = lax.all_gather(routing, "expert", axis=0, tiled=True)
    return rows, routing


def dense_gradient(rows, routing, up_full, expert):
    top_count = routing.shape[1] // 2
    all_gates, all_ids = routing[:, :top_count], routing[:, top_count:]
    chosen = all_ids == expert.astype(jnp.float32)
    weights_row = jnp.sum(jnp.where(chosen, all_gates, jnp.float32(0.0)), axis=1)
    scaled = (weights_row[:, None] * rows[1].astype(jnp.float32)).astype(jnp.bfloat16)
    hidden = jax.nn.silu(
        jnp.dot(rows[0], up_full, preferred_element_type=jnp.float32)
    ).astype(jnp.bfloat16)
    hidden = lax.optimization_barrier(hidden)
    return lax.dot_general(
        hidden, scaled, (((0,), (0,)), ((), ())), preferred_element_type=jnp.float32
    )


def grid_reduce_scatter(halves):
    where = lax.axis_index("dp")
    low, high = where % 2, where // 2
    size = lax.axis_size("dp")
    flip_low = [(d, d ^ 1) for d in range(size)]
    flip_high = [(d, d ^ 2) for d in range(size)]
    first, second = (half.reshape((2, 2, -1) + half.shape[1:]) for half in halves)
    sent = lax.ppermute(jnp.take(first, 1 - low, axis=1), "dp", flip_low)
    first = jnp.take(first, low, axis=1) + sent
    sent = lax.ppermute(jnp.take(second, 1 - high, axis=0), "dp", flip_high)
    second = jnp.take(second, high, axis=0) + sent
    sent = lax.ppermute(jnp.take(first, 1 - high, axis=0), "dp", flip_high)
    first = jnp.take(first, high, axis=0) + sent
    sent = lax.ppermute(jnp.take(second, 1 - low, axis=0), "dp", flip_low)
    second = jnp.take(second, low, axis=0) + sent
    return jnp.concatenate((first, second), axis=1)


def lamb_step(weight, moment_one, moment_two, gradient):
    first = beta_one * moment_one + (1.0 - beta_one) * gradient
    second = beta_two * moment_two + (1.0 - beta_two) * gradient * gradient
    update = first / (jnp.sqrt(second) + epsilon)
    weight_sq, update_sq = lax.psum((jnp.sum(weight * weight), jnp.sum(update * update)), "dp")
    trust_ratio = jnp.sqrt(weight_sq) / (jnp.sqrt(update_sq) + epsilon)
    renewed = weight - learn_rate * trust_ratio * update
    return (renewed, first, second)


def local(
    tokens, cotangent, expert_ids, gate_probs, up_weight, down_weight, moment1, moment2, pair_match
):
    group_size = lax.axis_size("expert")
    partner = pair_match[lax.axis_index("expert")]
    if group_size <= exchange_group_max and group_size * tokens.shape[0] <= dense_rows_max:
        rows, routing = gather_group(tokens, cotangent, expert_ids, gate_probs)
        routing, up_held = lax.optimization_barrier((routing, up_weight[0]))
        (up_local,) = exchange((up_held,), pair_match)
        up_local, held_weight = lax.optimization_barrier((up_local, down_weight[0]))
        (weight,) = exchange((held_weight,), pair_match)
        rows, up_ready = lax.optimization_barrier((rows, up_local))
        up_full = lax.all_gather(up_ready, "dp", axis=1, tiled=True)
        up_full, weight = lax.optimization_barrier((up_full, weight))
        partial = dense_gradient(rows, routing, up_full, partner)
        moments, partial = lax.optimization_barrier(((moment1[0], moment2[0]), partial))
        (swapped,) = exchange((jnp.stack(moments),), pair_match)
        moment_one, moment_two = swapped[0], swapped[1]
        gradient = lax.psum_scatter(partial, "dp", scatter_dimension=0, tiled=True)
    else:
        up_local = relocate(up_weight[0], pair_match)
        up_full = lax.all_gather(up_local, "dp", axis=1, tiled=True)
        partial = routed_gradient(tokens, cotangent, pair_match[expert_ids], gate_probs, up_full)
        weight, moment_one, moment_two = (
            relocate(x[0], pair_match) for x in (down_weight, moment1, moment2)
        )
        if lax.axis_size("dp") == 4 and partial.shape[0] % 4 == 0:
            middle = partial.shape[1] // 2
            gradient = grid_reduce_scatter((partial[:, :middle], partial[:, middle:]))
        else:
            gradient = lax.psum_scatter(partial, "dp", scatter_dimension=0, tiled=True)
    renewed, first, second = lamb_step(weight, moment_one, moment_two, gradient)
    return (renewed[None], first[None], second[None])


def solution(mesh):
    in_specs = (
        P(("dp", "expert"), None),
        P(("dp", "expert"), None),
        P(("dp", "expert"), None),
        P(("dp", "expert"), None),
        P("expert", None, "dp"),
        P("expert", "dp", None),
        P("expert", "dp", None),
        P("expert", "dp", None),
        P(),
    )
    out_specs = (P("expert", "dp", None), P("expert", "dp", None), P("expert", "dp", None))
    return jax.shard_map(local, mesh=mesh, in_specs=in_specs, out_specs=out_specs, check_vma=False)
```

```python
import jax
import jax.numpy as jnp
from jax import lax
from jax.sharding import PartitionSpec as P

beta_one = 0.9
beta_two = 0.999
epsilon = 1e-06
learn_rate = 0.05

dense_rows_max = 2048
exchange_group_max = 8


def relocate(state, pair_match):
    group_size = lax.axis_size("expert")
    pieces = state.reshape((group_size, -1) + state.shape[1:])
    spread = lax.all_to_all(pieces, "expert", split_axis=0, concat_axis=0, tiled=True)
    chosen = jnp.take(spread, pair_match, axis=0)
    arrived = lax.all_to_all(chosen, "expert", split_axis=0, concat_axis=0, tiled=True)
    return arrived.reshape(state.shape)


def perfect_matchings(members):
    if not members:
        return [()]
    first, rest = members[0], members[1:]
    found = []
    for at, other in enumerate(rest):
        for tail in perfect_matchings(rest[:at] + rest[at + 1 :]):
            found.append(((first, other),) + tail)
    return found


def exchange(states, pair_match):
    group_size = lax.axis_size("expert")
    matchings = perfect_matchings(tuple(range(group_size)))
    scale = [group_size**place for place in range(group_size)]
    keys = [sum(scale[a] * b + scale[b] * a for a, b in pairs) for pairs in matchings]
    key = jnp.sum(pair_match * jnp.array(scale, jnp.int32))
    branch = jnp.argmax(jnp.array(keys, jnp.int32) == key).astype(jnp.int32)

    def swap(pairs):
        perm = [(a, b) for a, b in pairs] + [(b, a) for a, b in pairs]
        return lambda values: tuple(lax.ppermute(value, "expert", perm) for value in values)

    return lax.switch(branch, [swap(pairs) for pairs in matchings], tuple(states))


def routed_gradient(tokens, cotangent, dest_ids, gate_probs, up_full):
    group_size = lax.axis_size("expert")
    tok_rows, top_count = dest_ids.shape
    width = tokens.shape[1]
    capacity = 3 * tok_rows * top_count // (2 * group_size)
    total = tok_rows * top_count
    flat_ids = dest_ids.reshape(-1)
    picked = (flat_ids[:, None] == jnp.arange(group_size, dtype=jnp.int32)[None, :]).astype(
        jnp.int32
    )
    ranking = jnp.sum((jnp.cumsum(picked, axis=0) - 1) * picked, axis=1)
    slot_index = flat_ids * capacity + ranking
    source = (
        jnp.full((group_size * capacity,), total, jnp.int32)
        .at[slot_index]
        .set(jnp.arange(total, dtype=jnp.int32))
    )
    filled = source < total
    safe_source = jnp.minimum(source, total - 1)
    row_index = safe_source // top_count
    weights_row = jnp.where(filled, gate_probs.reshape(-1)[safe_source], jnp.float32(0.0))
    sent_tokens = jnp.where(filled[:, None], tokens[row_index], jnp.zeros((), jnp.bfloat16))
    sent_scaled = (weights_row[:, None] * cotangent[row_index].astype(jnp.float32)).astype(
        jnp.bfloat16
    )
    sent_tokens = sent_tokens.reshape(group_size, capacity, width)
    sent_scaled = sent_scaled.reshape(group_size, capacity, width)
    got_tokens, got_scaled = (
        lax.all_to_all(sent_tokens, "expert", split_axis=0, concat_axis=0, tiled=True),
        lax.all_to_all(sent_scaled, "expert", split_axis=0, concat_axis=0, tiled=True),
    )
    rows_tokens = got_tokens.reshape(-1, width)
    rows_scaled = got_scaled.reshape(-1, width)
    hidden = jax.nn.silu(
        jnp.dot(rows_tokens, up_full, preferred_element_type=jnp.float32)
    ).astype(jnp.bfloat16)
    return lax.dot_general(
        hidden, rows_scaled, (((0,), (0,)), ((), ())), preferred_element_type=jnp.float32
    )


def gather_group(tokens, cotangent, expert_ids, gate_probs):
    rows = lax.all_gather(jnp.stack((tokens, cotangent)), "expert", axis=1, tiled=True)
    routing = jnp.concatenate((gate_probs, expert_ids.astype(jnp.float32)), axis=1)
    routing = lax.all_gather(routing, "expert", axis=0, tiled=True)
    return rows, routing


def dense_gradient(rows, routing, up_full, expert):
    top_count = routing.shape[1] // 2
    all_gates, all_ids = routing[:, :top_count], routing[:, top_count:]
    chosen = all_ids == expert.astype(jnp.float32)
    weights_row = jnp.sum(jnp.where(chosen, all_gates, jnp.float32(0.0)), axis=1)
    scaled = (weights_row[:, None] * rows[1].astype(jnp.float32)).astype(jnp.bfloat16)
    scaled = lax.optimization_barrier(scaled)
    hidden = jax.nn.silu(
        jnp.dot(rows[0], up_full, preferred_element_type=jnp.float32)
    ).astype(jnp.bfloat16)
    hidden = lax.optimization_barrier(hidden)
    return lax.dot_general(
        hidden, scaled, (((0,), (0,)), ((), ())), preferred_element_type=jnp.float32
    )


def grid_reduce_scatter(halves):
    where = lax.axis_index("dp")
    low, high = where % 2, where // 2
    size = lax.axis_size("dp")
    flip_low = [(d, d ^ 1) for d in range(size)]
    flip_high = [(d, d ^ 2) for d in range(size)]
    first, second = (half.reshape((2, 2, -1) + half.shape[1:]) for half in halves)
    sent = lax.ppermute(jnp.take(first, 1 - low, axis=1), "dp", flip_low)
    first = jnp.take(first, low, axis=1) + sent
    sent = lax.ppermute(jnp.take(second, 1 - high, axis=0), "dp", flip_high)
    second = jnp.take(second, high, axis=0) + sent
    sent = lax.ppermute(jnp.take(first, 1 - high, axis=0), "dp", flip_high)
    first = jnp.take(first, high, axis=0) + sent
    sent = lax.ppermute(jnp.take(second, 1 - low, axis=0), "dp", flip_low)
    second = jnp.take(second, low, axis=0) + sent
    return jnp.concatenate((first, second), axis=1)


def lamb_step(weight, moment_one, moment_two, gradient):
    first = beta_one * moment_one + (1.0 - beta_one) * gradient
    second = beta_two * moment_two + (1.0 - beta_two) * gradient * gradient
    update = first / (jnp.sqrt(second) + epsilon)
    weight_sq, update_sq = lax.psum((jnp.sum(weight * weight), jnp.sum(update * update)), "dp")
    trust_ratio = jnp.sqrt(weight_sq) / (jnp.sqrt(update_sq) + epsilon)
    renewed = weight - learn_rate * trust_ratio * update
    return (renewed, first, second)


def local(
    tokens, cotangent, expert_ids, gate_probs, up_weight, down_weight, moment1, moment2, pair_match
):
    group_size = lax.axis_size("expert")
    partner = pair_match[lax.axis_index("expert")]
    if group_size <= exchange_group_max and group_size * tokens.shape[0] <= dense_rows_max:
        rows, routing = gather_group(tokens, cotangent, expert_ids, gate_probs)
        routing, up_held = lax.optimization_barrier((routing, up_weight[0]))
        (up_local,) = exchange((up_held,), pair_match)
        up_local, held_weight = lax.optimization_barrier((up_local, down_weight[0]))
        (weight,) = exchange((held_weight,), pair_match)
        rows, up_ready = lax.optimization_barrier((rows, up_local))
        up_full = lax.all_gather(up_ready, "dp", axis=1, tiled=True)
        up_full, weight = lax.optimization_barrier((up_full, weight))
        partial = dense_gradient(rows, routing, up_full, partner)
        moments, partial = lax.optimization_barrier(((moment1[0], moment2[0]), partial))
        (swapped,) = exchange((jnp.stack(moments),), pair_match)
        moment_one, moment_two = swapped[0], swapped[1]
        gradient = lax.psum_scatter(partial, "dp", scatter_dimension=0, tiled=True)
    else:
        up_local = relocate(up_weight[0], pair_match)
        up_full = lax.all_gather(up_local, "dp", axis=1, tiled=True)
        partial = routed_gradient(tokens, cotangent, pair_match[expert_ids], gate_probs, up_full)
        weight, moment_one, moment_two = (
            relocate(x[0], pair_match) for x in (down_weight, moment1, moment2)
        )
        if lax.axis_size("dp") == 4 and partial.shape[0] % 4 == 0:
            middle = partial.shape[1] // 2
            gradient = grid_reduce_scatter((partial[:, :middle], partial[:, middle:]))
        else:
            gradient = lax.psum_scatter(partial, "dp", scatter_dimension=0, tiled=True)
    renewed, first, second = lamb_step(weight, moment_one, moment_two, gradient)
    return (renewed[None], first[None], second[None])


def solution(mesh):
    in_specs = (
        P(("dp", "expert"), None),
        P(("dp", "expert"), None),
        P(("dp", "expert"), None),
        P(("dp", "expert"), None),
        P("expert", None, "dp"),
        P("expert", "dp", None),
        P("expert", "dp", None),
        P("expert", "dp", None),
        P(),
    )
    out_specs = (P("expert", "dp", None), P("expert", "dp", None), P("expert", "dp", None))
    return jax.shard_map(local, mesh=mesh, in_specs=in_specs, out_specs=out_specs, check_vma=False)
```

```python
import jax
import jax.numpy as jnp
from jax import lax
from jax.sharding import PartitionSpec as P

beta_one = 0.9
beta_two = 0.999
epsilon = 1e-06
learn_rate = 0.05

dense_rows_max = 2048
exchange_group_max = 8


def relocate(state, pair_match):
    group_size = lax.axis_size("expert")
    pieces = state.reshape((group_size, -1) + state.shape[1:])
    spread = lax.all_to_all(pieces, "expert", split_axis=0, concat_axis=0, tiled=True)
    chosen = jnp.take(spread, pair_match, axis=0)
    arrived = lax.all_to_all(chosen, "expert", split_axis=0, concat_axis=0, tiled=True)
    return arrived.reshape(state.shape)


def perfect_matchings(members):
    if not members:
        return [()]
    first, rest = members[0], members[1:]
    found = []
    for at, other in enumerate(rest):
        for tail in perfect_matchings(rest[:at] + rest[at + 1 :]):
            found.append(((first, other),) + tail)
    return found


def exchange(states, pair_match):
    group_size = lax.axis_size("expert")
    matchings = perfect_matchings(tuple(range(group_size)))
    scale = [group_size**place for place in range(group_size)]
    keys = [sum(scale[a] * b + scale[b] * a for a, b in pairs) for pairs in matchings]
    key = jnp.sum(pair_match * jnp.array(scale, jnp.int32))
    branch = jnp.argmax(jnp.array(keys, jnp.int32) == key).astype(jnp.int32)

    def swap(pairs):
        perm = [(a, b) for a, b in pairs] + [(b, a) for a, b in pairs]
        return lambda values: tuple(lax.ppermute(value, "expert", perm) for value in values)

    return lax.switch(branch, [swap(pairs) for pairs in matchings], tuple(states))


def routed_gradient(tokens, cotangent, dest_ids, gate_probs, up_full):
    group_size = lax.axis_size("expert")
    tok_rows, top_count = dest_ids.shape
    width = tokens.shape[1]
    capacity = 3 * tok_rows * top_count // (2 * group_size)
    total = tok_rows * top_count
    flat_ids = dest_ids.reshape(-1)
    picked = (flat_ids[:, None] == jnp.arange(group_size, dtype=jnp.int32)[None, :]).astype(
        jnp.int32
    )
    ranking = jnp.sum((jnp.cumsum(picked, axis=0) - 1) * picked, axis=1)
    slot_index = flat_ids * capacity + ranking
    source = (
        jnp.full((group_size * capacity,), total, jnp.int32)
        .at[slot_index]
        .set(jnp.arange(total, dtype=jnp.int32))
    )
    filled = source < total
    safe_source = jnp.minimum(source, total - 1)
    row_index = safe_source // top_count
    weights_row = jnp.where(filled, gate_probs.reshape(-1)[safe_source], jnp.float32(0.0))
    sent_tokens = jnp.where(filled[:, None], tokens[row_index], jnp.zeros((), jnp.bfloat16))
    sent_scaled = (weights_row[:, None] * cotangent[row_index].astype(jnp.float32)).astype(
        jnp.bfloat16
    )
    sent_tokens = sent_tokens.reshape(group_size, capacity, width)
    sent_scaled = sent_scaled.reshape(group_size, capacity, width)
    got_tokens, got_scaled = (
        lax.all_to_all(sent_tokens, "expert", split_axis=0, concat_axis=0, tiled=True),
        lax.all_to_all(sent_scaled, "expert", split_axis=0, concat_axis=0, tiled=True),
    )
    rows_tokens = got_tokens.reshape(-1, width)
    rows_scaled = got_scaled.reshape(-1, width)
    hidden = jax.nn.silu(
        jnp.dot(rows_tokens, up_full, preferred_element_type=jnp.float32)
    ).astype(jnp.bfloat16)
    return lax.dot_general(
        hidden, rows_scaled, (((0,), (0,)), ((), ())), preferred_element_type=jnp.float32
    )


def gather_group(tokens, cotangent, expert_ids, gate_probs):
    rows = lax.all_gather(jnp.stack((tokens, cotangent)), "expert", axis=1, tiled=True)
    routing = jnp.concatenate((gate_probs, expert_ids.astype(jnp.float32)), axis=1)
    routing = lax.all_gather(routing, "expert", axis=0, tiled=True)
    return rows, routing


def dense_gradient(rows, routing, up_full, expert):
    top_count = routing.shape[1] // 2
    all_gates, all_ids = routing[:, :top_count], routing[:, top_count:]
    chosen = all_ids == expert.astype(jnp.float32)
    weights_row = jnp.sum(jnp.where(chosen, all_gates, jnp.float32(0.0)), axis=1)
    scaled = (weights_row[:, None] * rows[1].astype(jnp.float32)).astype(jnp.bfloat16)
    hidden = jax.nn.silu(
        jnp.dot(rows[0], up_full, preferred_element_type=jnp.float32)
    ).astype(jnp.bfloat16)
    hidden = lax.optimization_barrier(hidden)
    return lax.dot_general(
        hidden, scaled, (((0,), (0,)), ((), ())), preferred_element_type=jnp.float32
    )


def grid_reduce_scatter(halves):
    where = lax.axis_index("dp")
    low, high = where % 2, where // 2
    size = lax.axis_size("dp")
    flip_low = [(d, d ^ 1) for d in range(size)]
    flip_high = [(d, d ^ 2) for d in range(size)]
    first, second = (half.reshape((2, 2, -1) + half.shape[1:]) for half in halves)
    sent = lax.ppermute(jnp.take(first, 1 - low, axis=1), "dp", flip_low)
    first = jnp.take(first, low, axis=1) + sent
    sent = lax.ppermute(jnp.take(second, 1 - high, axis=0), "dp", flip_high)
    second = jnp.take(second, high, axis=0) + sent
    sent = lax.ppermute(jnp.take(first, 1 - high, axis=0), "dp", flip_high)
    first = jnp.take(first, high, axis=0) + sent
    sent = lax.ppermute(jnp.take(second, 1 - low, axis=0), "dp", flip_low)
    second = jnp.take(second, low, axis=0) + sent
    return jnp.concatenate((first, second), axis=1)


def lamb_step(weight, moment_one, moment_two, gradient):
    first = beta_one * moment_one + (1.0 - beta_one) * gradient
    second = beta_two * moment_two + (1.0 - beta_two) * gradient * gradient
    update = first / (jnp.sqrt(second) + epsilon)
    weight_sq, update_sq = lax.psum((jnp.sum(weight * weight), jnp.sum(update * update)), "dp")
    trust_ratio = jnp.sqrt(weight_sq) / (jnp.sqrt(update_sq) + epsilon)
    renewed = weight - learn_rate * trust_ratio * update
    return (renewed, first, second)


def local(
    tokens, cotangent, expert_ids, gate_probs, up_weight, down_weight, moment1, moment2, pair_match
):
    group_size = lax.axis_size("expert")
    partner = pair_match[lax.axis_index("expert")]
    if group_size <= exchange_group_max and group_size * tokens.shape[0] <= dense_rows_max:
        rows, routing = gather_group(tokens, cotangent, expert_ids, gate_probs)
        routing, up_held = lax.optimization_barrier((routing, up_weight[0]))
        (up_local,) = exchange((up_held,), pair_match)
        moments = jnp.stack((moment1[0], moment2[0]))
        up_local, held_weight, moments = lax.optimization_barrier((up_local, down_weight[0], moments))
        (weight,) = exchange((held_weight,), pair_match)
        rows, up_ready = lax.optimization_barrier((rows, up_local))
        up_full = lax.all_gather(up_ready, "dp", axis=1, tiled=True)
        up_full, weight = lax.optimization_barrier((up_full, weight))
        partial = dense_gradient(rows, routing, up_full, partner)
        moments, partial = lax.optimization_barrier((moments, partial))
        (swapped,) = exchange((moments,), pair_match)
        moment_one, moment_two = swapped[0], swapped[1]
        gradient = lax.psum_scatter(partial, "dp", scatter_dimension=0, tiled=True)
    else:
        up_local = relocate(up_weight[0], pair_match)
        up_full = lax.all_gather(up_local, "dp", axis=1, tiled=True)
        partial = routed_gradient(tokens, cotangent, pair_match[expert_ids], gate_probs, up_full)
        weight, moment_one, moment_two = (
            relocate(x[0], pair_match) for x in (down_weight, moment1, moment2)
        )
        if lax.axis_size("dp") == 4 and partial.shape[0] % 4 == 0:
            middle = partial.shape[1] // 2
            gradient = grid_reduce_scatter((partial[:, :middle], partial[:, middle:]))
        else:
            gradient = lax.psum_scatter(partial, "dp", scatter_dimension=0, tiled=True)
    renewed, first, second = lamb_step(weight, moment_one, moment_two, gradient)
    return (renewed[None], first[None], second[None])


def solution(mesh):
    in_specs = (
        P(("dp", "expert"), None),
        P(("dp", "expert"), None),
        P(("dp", "expert"), None),
        P(("dp", "expert"), None),
        P("expert", None, "dp"),
        P("expert", "dp", None),
        P("expert", "dp", None),
        P("expert", "dp", None),
        P(),
    )
    out_specs = (P("expert", "dp", None), P("expert", "dp", None), P("expert", "dp", None))
    return jax.shard_map(local, mesh=mesh, in_specs=in_specs, out_specs=out_specs, check_vma=False)
```
